256 devices in a mesh: space: 16 (over x, y), mode: 16 (over z, core).
Axes of the slice: x: 4, y: 4, z: 8, core: 2. Of those that a mesh axis runs over, the one named last changes fastest.
Arguments:
- density: float32 [512, 32, 256], P('mode', 'space'), may hold values from -6 to 6
- tensor: bfloat16 [512, 512, 512], P('mode', 'space'), may hold values from -0.01171875 to 0.01171875
- velocity: float32 [3, 512], P(None, 'mode'), may hold values from -1 to 1
- inflow: float32 [512], P('mode'), may hold values from -6 to 6
- flags: int32 [2, 256], replicated, may hold values 0 or 1
Outputs:
- collided: float32 [512, 32, 256], P('mode', 'space')
The draws below stay inside these ranges and needn't reach their ends.
All inputs are finite; a program needn't handle non-finite values.
Results may differ from the reference program's by a relative error of at most 0.0025.
Values may be sent and summed in bfloat16 or wider, within the bound.
No kernel may reach another device: no remote copies, remote signals or barrier semaphores. Data moves between devices by JAX's collectives and lax.ppermute only.
A program may use at most 128 MiB of HBM per device.

```python
import jax
import jax.numpy as jnp
from jax import lax

M = 512
NXY = 16
SUBSTEPS = 3
NZ = 32
XY = 256


def plant(entries, rng, low, high):
    spot = [jax.random.randint(jax.random.fold_in(rng, axis), (), 0, length) for axis, length in enumerate(entries.shape)]
    widest = entries.shape.index(max(entries.shape))
    next_to = spot[:widest] + [(spot[widest] + 1) % entries.shape[widest]] + spot[widest + 1:]
    return entries.at[tuple(spot)].set(low).at[tuple(next_to)].set(high)


def steps_of(own_key, extent, pieces, low, high):
    def one(position, shards_of):
        draws = jax.random.uniform(jax.random.fold_in(jax.random.fold_in(own_key, 6), position), (shards_of,), jnp.float32, low / len(pieces), high / len(pieces))
        return jnp.repeat(jnp.exp(draws), extent[position] // shards_of).reshape((-1,) + (1,) * (len(extent) - position - 1))

    level = one(*pieces[0])
    for cut in pieces[1:]:
        level = level * one(*cut)
    return level


def gaussian(key, shape, width, most, cuts=(), dtype=jnp.bfloat16):
    entries = width * jax.random.normal(key, shape, jnp.float32)
    if cuts:
        entries = entries * steps_of(key, shape, cuts, -0.22, 0.18)
    return jnp.clip(entries, -most, most).astype(dtype)


def setup_inputs(seed: int = 0) -> dict:
    arg_keys = jax.random.split(jax.random.key(seed), 6)
    density = gaussian(arg_keys[0], (M, NZ, XY), 1.0, 6.0, ((0, 16), (1, 16)), jnp.float32)
    tensor = gaussian(arg_keys[1], (M, M, M), (M * M) ** -0.5, 0.01171875, ((0, 16), (1, 16)))
    velocity = jnp.clip(jax.random.uniform(arg_keys[2], (3, M), jnp.float32, -1.0, 1.0) * steps_of(arg_keys[2], (3, M), ((1, 16),), -0.4, 0.0), -1.0, 1.0)
    inflow = gaussian(arg_keys[3], (M,), 1.0, 6.0, ((0, 16),), jnp.float32)
    flags = plant((jax.random.randint(arg_keys[4], (2, XY), 0, 2) < 1).astype(jnp.int32), jax.random.fold_in(arg_keys[4], 1), 0, 1)
    return {"density": density, "tensor": tensor, "velocity": velocity, "inflow": inflow, "flags": flags}


courant = 0.3
time_step = 0.5


def neighbours(field):
    rows, planes, cells = field.shape
    grid = field.reshape(rows, planes, NXY, NXY)
    padded = jnp.pad(grid, ((0, 0), (0, 0), (1, 1), (1, 1)))
    lower_x = padded[:, :, :-2, 1:-1].reshape(field.shape)
    upper_x = padded[:, :, 2:, 1:-1].reshape(field.shape)
    lower_y = padded[:, :, 1:-1, :-2].reshape(field.shape)
    upper_y = padded[:, :, 1:-1, 2:].reshape(field.shape)
    return lower_x, upper_x, lower_y, upper_y


def upwind(field, below, above, velocity):
    lower_x, upper_x, lower_y, upper_y = neighbours(field)
    lowers = [lower_x, lower_y, below]
    uppers = [upper_x, upper_y, above]
    flux = jnp.zeros_like(field)
    for direction in range(3):
        speed = velocity[direction][:, None, None]
        flux = flux + jnp.maximum(speed, 0.0) * (field - lowers[direction])
        flux = flux + jnp.minimum(speed, 0.0) * (uppers[direction] - field)
    return field - courant * flux


def reference(density, tensor, velocity, inflow, flags):
    ghost_low = flags[0].astype(jnp.float32)[None, :] * inflow[:, None]
    ghost_high = flags[1].astype(jnp.float32)[None, :] * inflow[:, None]
    field = density
    for substep in range(SUBSTEPS):
        padded = jnp.concatenate([ghost_low[:, None, :], field, ghost_high[:, None, :]], axis=1)
        field = upwind(field, padded[:, :-2], padded[:, 2:], velocity)
    coarse = field.astype(jnp.bfloat16)
    columns = coarse.reshape(M, -1).astype(jnp.float32)
    blocks = tensor.reshape(M // 16, 16, M, M)

    def one_block(block):
        inner = jnp.dot(block.astype(jnp.float32).reshape(16 * M, M), columns, precision=lax.Precision.HIGHEST)
        return jnp.sum(inner.reshape(16, M, -1) * columns[None], axis=1)

    gain = lax.map(one_block, blocks).reshape(field.shape)
    return field + time_step * gain
```

```python
import functools

import jax
import jax.numpy as jnp
from jax import lax
from jax.experimental import pallas as pl
from jax.experimental.pallas import tpu as pltpu
from jax.sharding import Mesh
from jax.sharding import PartitionSpec as P

NXY = 16
SUBSTEPS = 3
HALO = SUBSTEPS

courant = 0.3
time_step = 0.5

SPACE = ("sx", "sy")
MODE = ("mz", "mc")


def neighbours(field):
    rows, planes, cells = field.shape
    grid = field.reshape(rows, planes, NXY, NXY)
    padded = jnp.pad(grid, ((0, 0), (0, 0), (1, 1), (1, 1)))
    lower_x = padded[:, :, :-2, 1:-1].reshape(field.shape)
    upper_x = padded[:, :, 2:, 1:-1].reshape(field.shape)
    lower_y = padded[:, :, 1:-1, :-2].reshape(field.shape)
    upper_y = padded[:, :, 1:-1, 2:].reshape(field.shape)
    return (lower_x, upper_x, lower_y, upper_y)


def upwind(field, below, above, velocity):
    lower_x, upper_x, lower_y, upper_y = neighbours(field)
    lowers = [lower_x, lower_y, below]
    uppers = [upper_x, upper_y, above]
    flux = jnp.zeros_like(field)
    for direction in range(3):
        speed = velocity[direction][:, None, None]
        flux = flux + jnp.maximum(speed, 0.0) * (field - lowers[direction])
        flux = flux + jnp.minimum(speed, 0.0) * (uppers[direction] - field)
    return field - courant * flux


def shifted(block, count, distance, planes):
    if distance > 0:
        pairs = [(i, i + distance) for i in range(count - distance)]
        piece = block[:, block.shape[1] - planes :]
    else:
        pairs = [(i, i + distance) for i in range(-distance, count)]
        piece = block[:, :planes]
    return lax.ppermute(piece, SPACE, pairs)


def transport(density, velocity, ghost_low, ghost_high):
    count = lax.axis_size(SPACE)
    position = lax.axis_index(SPACE)
    depth = density.shape[1]
    total_planes = count * depth
    below, above = [], []
    need = HALO
    distance = 1
    while need > 0:
        take = min(need, depth)
        below.insert(0, shifted(density, count, distance, take))
        above.append(shifted(density, count, -distance, take))
        need -= take
        distance += 1
    ext = jnp.concatenate(below + [density] + above, axis=1)
    planes = ext.shape[1]
    z = position * depth - HALO + lax.broadcasted_iota(jnp.int32, (1, planes, 1), 1)
    low_mask = z < 0
    high_mask = z >= total_planes

    def fix(f):
        f = jnp.where(low_mask, ghost_low[:, None, :], f)
        return jnp.where(high_mask, ghost_high[:, None, :], f)

    field = fix(ext)
    for _ in range(SUBSTEPS):
        lower = jnp.concatenate([field[:, :1], field[:, :-1]], axis=1)
        upper = jnp.concatenate([field[:, 1:], field[:, -1:]], axis=1)
        field = fix(upwind(field, lower, upper, velocity))
    return field[:, HALO : HALO + depth]


def gain_kernel(t_ref, x_ref, xi_ref, o_ref, *, group, rows):
    x = x_ref[...]
    xi = xi_ref[...].astype(jnp.float32)
    n_groups = o_ref.shape[0] // group

    def body(g, carry):
        start = pl.multiple_of(g * group * rows, group * rows)
        t = t_ref[pl.ds(start, group * rows), :]
        inner = jnp.dot(t, x, preferred_element_type=jnp.float32)
        inner = inner.reshape(group, rows, inner.shape[-1])
        o_ref[pl.ds(pl.multiple_of(g * group, group), group), :] = jnp.sum(
            inner * xi[None], axis=1
        )
        return carry

    lax.fori_loop(0, n_groups, body, 0)


def contract(tensor2d, columns, factor, k_count, tile=512, group=8):
    kr, width = tensor2d.shape
    rows = kr // k_count
    cells = columns.shape[1]
    kernel = functools.partial(gain_kernel, group=group, rows=rows)
    return pl.pallas_call(
        kernel,
        out_shape=jax.ShapeDtypeStruct((k_count, cells), jnp.float32),
        grid=(cells // tile,),
        in_specs=[
            pl.BlockSpec((kr, width), lambda c: (0, 0)),
            pl.BlockSpec((width, tile), lambda c: (0, c)),
            pl.BlockSpec((rows, tile), lambda c: (0, c)),
        ],
        out_specs=pl.BlockSpec((k_count, tile), lambda c: (0, c)),
        compiler_params=pltpu.CompilerParams(vmem_limit_bytes=48 * 1024 * 1024),
        cost_estimate=pl.CostEstimate(
            flops=2 * kr * width * cells + 2 * kr * cells,
            bytes_accessed=kr * width * 2 + width * cells * 2 + rows * cells * 2 + k_count * cells * 4,
            transcendentals=0,
        ),
    )(tensor2d, columns, factor)


def per_device(density, tensor, velocity, inflow, flags):
    rows, depth, cells = density.shape
    ghost_low = flags[0].astype(jnp.float32)[None, :] * inflow[:, None]
    ghost_high = flags[1].astype(jnp.float32)[None, :] * inflow[:, None]

    pair_tensor = lax.all_gather(tensor, "mc", axis=0, tiled=True)

    field = transport(density, velocity, ghost_low, ghost_high)

    coarse = field.astype(jnp.bfloat16)
    mine = lax.all_to_all(coarse, "mc", 1, 0, tiled=True)
    mine = lax.all_gather(mine, "mz", axis=0, tiled=True)
    modes = mine.shape[0]
    columns = lax.all_gather(mine.reshape(modes, cells), SPACE, axis=1, tiled=True)

    k_count, i_count, width = pair_tensor.shape
    position = lax.axis_index(SPACE)
    factor = lax.dynamic_slice_in_dim(columns, position * i_count, i_count, axis=0)
    partial = contract(pair_tensor.reshape(k_count * i_count, width), columns, factor, k_count)

    count = lax.axis_size(SPACE)
    partial = partial.reshape(k_count, count, cells)
    gain = lax.psum_scatter(partial, SPACE, scatter_dimension=1, tiled=True)
    gain = lax.all_to_all(gain, "mc", 0, 1, tiled=True)
    return field + time_step * gain.reshape(field.shape)


def solution(mesh):
    devices = mesh.devices
    space, mode = devices.shape
    fine = Mesh(devices.reshape(4, space // 4, mode // 2, 2), SPACE + MODE)
    in_specs = (P(MODE, SPACE, None), P(MODE, SPACE, None), P(None, MODE), P(MODE), P())
    out_specs = P(MODE, SPACE, None)
    return jax.shard_map(
        per_device, mesh=fine, in_specs=in_specs, out_specs=out_specs, check_vma=False
    )
```

```python
import functools

import jax
import jax.numpy as jnp
from jax import lax
from jax.experimental import pallas as pl
from jax.experimental.pallas import tpu as pltpu
from jax.sharding import Mesh
from jax.sharding import PartitionSpec as P

NXY = 16
SUBSTEPS = 3
HALO = SUBSTEPS

courant = 0.3
time_step = 0.5

SPACE = ("sx", "sy")
MODE = ("mz", "mc")


def neighbours(field):
    rows, planes, cells = field.shape
    grid = field.reshape(rows, planes, NXY, NXY)
    padded = jnp.pad(grid, ((0, 0), (0, 0), (1, 1), (1, 1)))
    lower_x = padded[:, :, :-2, 1:-1].reshape(field.shape)
    upper_x = padded[:, :, 2:, 1:-1].reshape(field.shape)
    lower_y = padded[:, :, 1:-1, :-2].reshape(field.shape)
    upper_y = padded[:, :, 1:-1, 2:].reshape(field.shape)
    return (lower_x, upper_x, lower_y, upper_y)


def upwind(field, below, above, velocity):
    lower_x, upper_x, lower_y, upper_y = neighbours(field)
    lowers = [lower_x, lower_y, below]
    uppers = [upper_x, upper_y, above]
    flux = jnp.zeros_like(field)
    for direction in range(3):
        speed = velocity[direction][:, None, None]
        flux = flux + jnp.maximum(speed, 0.0) * (field - lowers[direction])
        flux = flux + jnp.minimum(speed, 0.0) * (uppers[direction] - field)
    return field - courant * flux


def with_halo(block, sides, width):
    for axis, dim in sides:
        count = lax.axis_size(axis)
        forward = [(i, i + 1) for i in range(count - 1)]
        backward = [(target, source) for source, target in forward]
        low = lax.ppermute(
            lax.slice_in_dim(block, block.shape[dim] - width, None, axis=dim), axis, forward
        )
        high = lax.ppermute(lax.slice_in_dim(block, 0, width, axis=dim), axis, backward)
        block = jnp.concatenate([low, block, high], axis=dim)
    return block


def gain_kernel(t_ref, x_ref, xi_ref, o_ref, *, group, rows):
    z, _, jz, tile = x_ref.shape
    x = x_ref[...].reshape(z * jz, tile)
    xi = xi_ref[0].astype(jnp.float32)
    n_groups = o_ref.shape[1] // group

    def body(g, carry):
        start = pl.multiple_of(g * group * rows, group * rows)
        t = t_ref[pl.ds(start, group * rows), :]
        inner = jnp.dot(t, x, preferred_element_type=jnp.float32)
        inner = inner.reshape(group, rows, tile)
        o_ref[0, pl.ds(pl.multiple_of(g * group, group), group), :] = jnp.sum(
            inner * xi[None], axis=1
        )
        return carry

    lax.fori_loop(0, n_groups, body, 0)


def contract(tensor2d, gathered, factor, k_count, group=8):
    kr, width = tensor2d.shape
    rows = kr // k_count
    z, slabs, jz, tile = gathered.shape
    kernel = functools.partial(gain_kernel, group=group, rows=rows)
    cells = slabs * tile
    return pl.pallas_call(
        kernel,
        out_shape=jax.ShapeDtypeStruct((slabs, k_count, tile), jnp.float32),
        grid=(slabs,),
        in_specs=[
            pl.BlockSpec((kr, width), lambda c: (0, 0)),
            pl.BlockSpec((z, 1, jz, tile), lambda c: (0, c, 0, 0)),
            pl.BlockSpec((1, rows, tile), lambda c: (c, 0, 0)),
        ],
        out_specs=pl.BlockSpec((1, k_count, tile), lambda c: (c, 0, 0)),
        compiler_params=pltpu.CompilerParams(vmem_limit_bytes=48 * 1024 * 1024),
        cost_estimate=pl.CostEstimate(
            flops=2 * kr * width * cells + 2 * kr * cells,
            bytes_accessed=kr * width * 2 + width * cells * 2 + rows * cells * 2 + k_count * cells * 4,
            transcendentals=0,
        ),
    )(tensor2d, gathered, factor)


def swap_pair(x):
    return lax.ppermute(x, "mc", [(0, 1), (1, 0)])


def in_core_order(first_core, mine, other, axis):
    a = jnp.concatenate([mine, other], axis=axis)
    b = jnp.concatenate([other, mine], axis=axis)
    return jnp.where(first_core, a, b)


def per_device(density, tensor, velocity, inflow, flags):
    rows, depth, cells = density.shape
    position = lax.axis_index(SPACE)
    final = lax.axis_size(SPACE) - 1
    ghost_low = flags[0].astype(jnp.float32)[None, :] * inflow[:, None]
    ghost_high = flags[1].astype(jnp.float32)[None, :] * inflow[:, None]
    core = lax.axis_index("mc")
    first_core = core == 0

    other_tensor = swap_pair(tensor)

    field = density
    for substep in range(SUBSTEPS):
        padded = with_halo(field, ((SPACE, 1),), 1)
        low_plane = jnp.where(position == 0, ghost_low, padded[:, 0])
        high_plane = jnp.where(position == final, ghost_high, padded[:, -1])
        below = jnp.concatenate([low_plane[:, None], padded[:, 1:-2]], axis=1)
        above = jnp.concatenate([padded[:, 2:-1], high_plane[:, None]], axis=1)
        field = upwind(field, below, above, velocity)

    coarse = field.astype(jnp.bfloat16)
    keep = jnp.where(first_core, coarse[:, 0], coarse[:, 1])
    send = jnp.where(first_core, coarse[:, 1], coarse[:, 0])
    mine = in_core_order(first_core, keep, swap_pair(send), 0)
    modes = mine.shape[0]
    gathered = lax.all_gather(mine, ("mz", "sx", "sy"), axis=0, tiled=False)
    z_count = lax.axis_size("mz")
    count = lax.axis_size(SPACE)
    gathered = gathered.reshape(z_count, count, modes, cells)

    k_own, i_count, width = tensor.shape
    pair_tensor = in_core_order(first_core, tensor, other_tensor, 0)
    k_count = 2 * k_own
    start = position * i_count
    factor = lax.dynamic_slice(
        gathered, (start // modes, 0, start % modes, 0), (1, count, i_count, cells)
    ).reshape(count, i_count, cells)
    partial = contract(pair_tensor.reshape(k_count * i_count, width), gathered, factor, k_count)

    slabs = partial.shape[0]
    gain = lax.psum_scatter(
        partial.reshape(slabs * k_count, cells), SPACE, scatter_dimension=0, tiled=True
    )
    own_k = jnp.where(first_core, gain[:k_own], gain[k_own:])
    other_k = jnp.where(first_core, gain[k_own:], gain[:k_own])
    gain = in_core_order(first_core, own_k[:, None], swap_pair(other_k)[:, None], 1)
    return field + time_step * gain


def solution(mesh):
    devices = mesh.devices
    space, mode = devices.shape
    fine = Mesh(devices.reshape(4, space // 4, mode // 2, 2), SPACE + MODE)
    in_specs = (P(MODE, SPACE, None), P(MODE, SPACE, None), P(None, MODE), P(MODE), P())
    out_specs = P(MODE, SPACE, None)
    return jax.shard_map(
        per_device, mesh=fine, in_specs=in_specs, out_specs=out_specs, check_vma=False
    )
```

```python
import functools

import jax
import jax.numpy as jnp
from jax import lax
from jax.experimental import pallas as pl
from jax.experimental.pallas import tpu as pltpu
from jax.sharding import Mesh
from jax.sharding import PartitionSpec as P

NXY = 16
SUBSTEPS = 3
HALO = SUBSTEPS

courant = 0.3
time_step = 0.5


SPACE = ("sx", "sy")
MODE = ("mz", "mc")


def neighbours(field):
    rows, planes, cells = field.shape
    grid = field.reshape(rows, planes, NXY, NXY)
    padded = jnp.pad(grid, ((0, 0), (0, 0), (1, 1), (1, 1)))
    lower_x = padded[:, :, :-2, 1:-1].reshape(field.shape)
    upper_x = padded[:, :, 2:, 1:-1].reshape(field.shape)
    lower_y = padded[:, :, 1:-1, :-2].reshape(field.shape)
    upper_y = padded[:, :, 1:-1, 2:].reshape(field.shape)
    return (lower_x, upper_x, lower_y, upper_y)


def upwind(field, below, above, velocity):
    lower_x, upper_x, lower_y, upper_y = neighbours(field)
    lowers = [lower_x, lower_y, below]
    uppers = [upper_x, upper_y, above]
    flux = jnp.zeros_like(field)
    for direction in range(3):
        speed = velocity[direction][:, None, None]
        flux = flux + jnp.maximum(speed, 0.0) * (field - lowers[direction])
        flux = flux + jnp.minimum(speed, 0.0) * (uppers[direction] - field)
    return field - courant * flux


def with_halo(block, sides, width):
    for axis, dim in sides:
        count = lax.axis_size(axis)
        forward = [(i, i + 1) for i in range(count - 1)]
        backward = [(target, source) for source, target in forward]
        low = lax.ppermute(
            lax.slice_in_dim(block, block.shape[dim] - width, None, axis=dim), axis, forward
        )
        high = lax.ppermute(lax.slice_in_dim(block, 0, width, axis=dim), axis, backward)
        block = jnp.concatenate([low, block, high], axis=dim)
    return block


def gain_kernel(t_ref, x_ref, xi_ref, o_ref, *, group, rows):
    x = x_ref[...]
    xi = xi_ref[...].astype(jnp.float32)
    pieces, k_count, cells = o_ref.shape
    n_groups = k_count // group

    def body(g, carry):
        start = pl.multiple_of(g * group * rows, group * rows)
        t = t_ref[pl.ds(start, group * rows), :]
        inner = jnp.dot(t, x, preferred_element_type=jnp.float32)
        inner = inner.reshape(group, rows, inner.shape[-1])
        out = jnp.sum(inner * xi[None], axis=1)
        for p in range(pieces):
            o_ref[p, pl.ds(pl.multiple_of(g * group, group), group), :] = out[:, p * cells : (p + 1) * cells]
        return carry

    lax.fori_loop(0, n_groups, body, 0)


def contract(tensor2d, columns, factor, k_count, cells, tile=512, group=8):
    kr, width = tensor2d.shape
    rows = kr // k_count
    total = columns.shape[1]
    kernel = functools.partial(gain_kernel, group=group, rows=rows)
    return pl.pallas_call(
        kernel,
        out_shape=jax.ShapeDtypeStruct((total // cells, k_count, cells), jnp.float32),
        grid=(total // tile,),
        in_specs=[
            pl.BlockSpec((kr, width), lambda c: (0, 0)),
            pl.BlockSpec((width, tile), lambda c: (0, c)),
            pl.BlockSpec((rows, tile), lambda c: (0, c)),
        ],
        out_specs=pl.BlockSpec((tile // cells, k_count, cells), lambda c: (c, 0, 0)),
        compiler_params=pltpu.CompilerParams(vmem_limit_bytes=48 * 1024 * 1024),
        cost_estimate=pl.CostEstimate(
            flops=2 * kr * width * total + 2 * kr * total,
            bytes_accessed=kr * width * 2 + width * total * 2 + rows * total * 2 + k_count * total * 4,
            transcendentals=0,
        ),
    )(tensor2d, columns, factor)


def ring_gather(x, axis):
    count = lax.axis_size(axis)
    me = lax.axis_index(axis)
    pieces = [x]
    for d in range(1, count):
        pieces.append(lax.ppermute(x, axis, [(i, (i + d) % count) for i in range(count)]))
    stacked = jnp.stack(pieces[::-1], axis=0)
    return jnp.roll(stacked, me + 1, axis=0)


def ring_reduce_scatter(pieces, axis):
    count = lax.axis_size(axis)
    me = lax.axis_index(axis)
    total = lax.dynamic_index_in_dim(pieces, me, axis=0, keepdims=False)
    for d in range(1, count):
        piece = lax.dynamic_index_in_dim(pieces, (me + d) % count, axis=0, keepdims=False)
        total = total + lax.ppermute(piece, axis, [(i, (i + d) % count) for i in range(count)])
    return total


def swap_pair(x):
    return lax.ppermute(x, "mc", [(0, 1), (1, 0)])


def in_core_order(first_core, mine, other, axis):
    a = jnp.concatenate([mine, other], axis=axis)
    b = jnp.concatenate([other, mine], axis=axis)
    return jnp.where(first_core, a, b)


def per_device(density, tensor, velocity, inflow, flags):
    rows, depth, cells = density.shape
    position = lax.axis_index(SPACE)
    final = lax.axis_size(SPACE) - 1
    ghost_low = flags[0].astype(jnp.float32)[None, :] * inflow[:, None]
    ghost_high = flags[1].astype(jnp.float32)[None, :] * inflow[:, None]
    core = lax.axis_index("mc")
    first_core = core == 0

    other_tensor = swap_pair(tensor)

    field = density
    for substep in range(SUBSTEPS):
        padded = with_halo(field, ((SPACE, 1),), 1)
        low_plane = jnp.where(position == 0, ghost_low, padded[:, 0])
        high_plane = jnp.where(position == final, ghost_high, padded[:, -1])
        below = jnp.concatenate([low_plane[:, None], padded[:, 1:-2]], axis=1)
        above = jnp.concatenate([padded[:, 2:-1], high_plane[:, None]], axis=1)
        field = upwind(field, below, above, velocity)

    coarse = field.astype(jnp.bfloat16)
    keep = jnp.where(first_core, coarse[:, 0], coarse[:, 1])
    send = jnp.where(first_core, coarse[:, 1], coarse[:, 0])
    mine = in_core_order(first_core, keep, swap_pair(send), 0)
    modes = mine.shape[0]
    z_count = lax.axis_size("mz")
    mine = ring_gather(mine, "mz").reshape(z_count * modes, cells)
    columns = lax.all_gather(mine, SPACE, axis=1, tiled=True)

    k_own, i_count, width = tensor.shape
    pair_tensor = in_core_order(first_core, tensor, other_tensor, 0)
    k_count = 2 * k_own
    factor = lax.dynamic_slice_in_dim(columns, position * i_count, i_count, axis=0)
    partial = contract(
        pair_tensor.reshape(k_count * i_count, width), columns, factor, k_count, cells
    )
    gain = ring_reduce_scatter(partial, SPACE)
    own_k = jnp.where(first_core, gain[:k_own], gain[k_own:])
    other_k = jnp.where(first_core, gain[k_own:], gain[:k_own])
    gain = in_core_order(first_core, own_k[:, None], swap_pair(other_k)[:, None], 1)
    return field + time_step * gain


def solution(mesh):
    devices = mesh.devices
    space, mode = devices.shape
    fine = Mesh(devices.reshape(4, space // 4, mode // 2, 2), SPACE + MODE)
    in_specs = (P(MODE, SPACE, None), P(MODE, SPACE, None), P(None, MODE), P(MODE), P())
    out_specs = P(MODE, SPACE, None)
    return jax.shard_map(
        per_device, mesh=fine, in_specs=in_specs, out_specs=out_specs, check_vma=False
    )
```

```python
import functools

import jax
import jax.numpy as jnp
from jax import lax
from jax.experimental import pallas as pl
from jax.experimental.pallas import tpu as pltpu
from jax.sharding import Mesh
from jax.sharding import PartitionSpec as P

NXY = 16
SUBSTEPS = 3
HALO = SUBSTEPS

courant = 0.3
time_step = 0.5


SPACE = ("sx", "sy")
MODE = ("mz", "mc")


def neighbours(field):
    rows, planes, cells = field.shape
    grid = field.reshape(rows, planes, NXY, NXY)
    padded = jnp.pad(grid, ((0, 0), (0, 0), (1, 1), (1, 1)))
    lower_x = padded[:, :, :-2, 1:-1].reshape(field.shape)
    upper_x = padded[:, :, 2:, 1:-1].reshape(field.shape)
    lower_y = padded[:, :, 1:-1, :-2].reshape(field.shape)
    upper_y = padded[:, :, 1:-1, 2:].reshape(field.shape)
    return (lower_x, upper_x, lower_y, upper_y)


def upwind(field, below, above, velocity):
    lower_x, upper_x, lower_y, upper_y = neighbours(field)
    lowers = [lower_x, lower_y, below]
    uppers = [upper_x, upper_y, above]
    flux = jnp.zeros_like(field)
    for direction in range(3):
        speed = velocity[direction][:, None, None]
        flux = flux + jnp.maximum(speed, 0.0) * (field - lowers[direction])
        flux = flux + jnp.minimum(speed, 0.0) * (uppers[direction] - field)
    return field - courant * flux


def with_halo(block, sides, width):
    for axis, dim in sides:
        count = lax.axis_size(axis)
        forward = [(i, i + 1) for i in range(count - 1)]
        backward = [(target, source) for source, target in forward]
        low = lax.ppermute(
            lax.slice_in_dim(block, block.shape[dim] - width, None, axis=dim), axis, forward
        )
        high = lax.ppermute(lax.slice_in_dim(block, 0, width, axis=dim), axis, backward)
        block = jnp.concatenate([low, block, high], axis=dim)
    return block


def gain_kernel(t_ref, x_ref, xi_ref, o_ref, *, group, rows):
    x = x_ref[...]
    xi = xi_ref[...].astype(jnp.float32)
    pieces, k_count, cells = o_ref.shape
    n_groups = k_count // group

    def body(g, carry):
        start = pl.multiple_of(g * group * rows, group * rows)
        t = t_ref[pl.ds(start, group * rows), :]
        inner = jnp.dot(t, x, preferred_element_type=jnp.float32)
        inner = inner.reshape(group, rows, inner.shape[-1])
        out = jnp.sum(inner * xi[None], axis=1)
        for p in range(pieces):
            o_ref[p, pl.ds(pl.multiple_of(g * group, group), group), :] = out[:, p * cells : (p + 1) * cells]
        return carry

    lax.fori_loop(0, n_groups, body, 0)


def contract(tensor2d, columns, factor, k_count, cells, tile=512, group=8):
    kr, width = tensor2d.shape
    rows = kr // k_count
    total = columns.shape[1]
    kernel = functools.partial(gain_kernel, group=group, rows=rows)
    return pl.pallas_call(
        kernel,
        out_shape=jax.ShapeDtypeStruct((total // cells, k_count, cells), jnp.float32),
        grid=(total // tile,),
        in_specs=[
            pl.BlockSpec((kr, width), lambda c: (0, 0)),
            pl.BlockSpec((width, tile), lambda c: (0, c)),
            pl.BlockSpec((rows, tile), lambda c: (0, c)),
        ],
        out_specs=pl.BlockSpec((tile // cells, k_count, cells), lambda c: (c, 0, 0)),
        compiler_params=pltpu.CompilerParams(vmem_limit_bytes=48 * 1024 * 1024),
        cost_estimate=pl.CostEstimate(
            flops=2 * kr * width * total + 2 * kr * total,
            bytes_accessed=kr * width * 2 + width * total * 2 + rows * total * 2 + k_count * total * 4,
            transcendentals=0,
        ),
    )(tensor2d, columns, factor)


def ring_gather(x, axis):
    count = lax.axis_size(axis)
    me = lax.axis_index(axis)
    pieces = [x]
    for d in range(1, count):
        pieces.append(lax.ppermute(x, axis, [(i, (i + d) % count) for i in range(count)]))
    stacked = jnp.stack(pieces[::-1], axis=0)
    return jnp.roll(stacked, me + 1, axis=0)


def ring_reduce_scatter(pieces, axis):
    count = lax.axis_size(axis)
    me = lax.axis_index(axis)
    total = lax.dynamic_index_in_dim(pieces, me, axis=0, keepdims=False)
    for d in range(1, count):
        piece = lax.dynamic_index_in_dim(pieces, (me + d) % count, axis=0, keepdims=False)
        total = total + lax.ppermute(piece, axis, [(i, (i + d) % count) for i in range(count)])
    return total


def swap_pair(x):
    return lax.ppermute(x, "mc", [(0, 1), (1, 0)])


def in_core_order(first_core, mine, other, axis):
    a = jnp.concatenate([mine, other], axis=axis)
    b = jnp.concatenate([other, mine], axis=axis)
    return jnp.where(first_core, a, b)


def per_device(density, tensor, velocity, inflow, flags):
    rows, depth, cells = density.shape
    position = lax.axis_index(SPACE)
    final = lax.axis_size(SPACE) - 1
    ghost_low = flags[0].astype(jnp.float32)[None, :] * inflow[:, None]
    ghost_high = flags[1].astype(jnp.float32)[None, :] * inflow[:, None]

    with jax.named_scope("tgather"):
        wide_tensor = lax.all_gather(tensor, "sy", axis=1, tiled=True)

    field = density
    for substep in range(SUBSTEPS):
        with jax.named_scope(f"substep{substep}"):
            padded = with_halo(field, ((SPACE, 1),), 1)
            low_plane = jnp.where(position == 0, ghost_low, padded[:, 0])
            high_plane = jnp.where(position == final, ghost_high, padded[:, -1])
            below = jnp.concatenate([low_plane[:, None], padded[:, 1:-2]], axis=1)
            above = jnp.concatenate([padded[:, 2:-1], high_plane[:, None]], axis=1)
            field = upwind(field, below, above, velocity)

    field, wide_tensor = lax.optimization_barrier((field, wide_tensor))
    coarse = field.astype(jnp.bfloat16)
    all_modes = lax.all_gather(coarse, MODE, axis=0, tiled=True)
    columns = lax.all_gather(all_modes, "sx", axis=1, tiled=True)
    modes = columns.shape[0]
    columns = columns.reshape(modes, -1)

    k_count, i_count, width = wide_tensor.shape
    sx = lax.axis_index("sx")
    factor = lax.dynamic_slice_in_dim(columns, sx * i_count, i_count, axis=0)
    partial = contract(
        wide_tensor.reshape(k_count * i_count, width), columns, factor, k_count, depth * cells
    )
    gain = ring_reduce_scatter(partial, "sx")
    return field + time_step * gain.reshape(field.shape)


def solution(mesh):
    devices = mesh.devices
    space, mode = devices.shape
    fine = Mesh(devices.reshape(4, space // 4, mode // 2, 2), SPACE + MODE)
    in_specs = (P(MODE, SPACE, None), P(MODE, SPACE, None), P(None, MODE), P(MODE), P())
    out_specs = P(MODE, SPACE, None)
    return jax.shard_map(
        per_device, mesh=fine, in_specs=in_specs, out_specs=out_specs, check_vma=False
    )
```

```python
import functools

import jax
import jax.numpy as jnp
from jax import lax
from jax.experimental import pallas as pl
from jax.experimental.pallas import tpu as pltpu
from jax.sharding import Mesh
from jax.sharding import PartitionSpec as P

NXY = 16
SUBSTEPS = 3
HALO = SUBSTEPS

courant = 0.3
time_step = 0.5


SPACE = ("sx", "sy")
MODE = ("mz", "mc")


def neighbours(field):
    rows, planes, cells = field.shape
    grid = field.reshape(rows, planes, NXY, NXY)
    padded = jnp.pad(grid, ((0, 0), (0, 0), (1, 1), (1, 1)))
    lower_x = padded[:, :, :-2, 1:-1].reshape(field.shape)
    upper_x = padded[:, :, 2:, 1:-1].reshape(field.shape)
    lower_y = padded[:, :, 1:-1, :-2].reshape(field.shape)
    upper_y = padded[:, :, 1:-1, 2:].reshape(field.shape)
    return (lower_x, upper_x, lower_y, upper_y)


def upwind(field, below, above, velocity):
    lower_x, upper_x, lower_y, upper_y = neighbours(field)
    lowers = [lower_x, lower_y, below]
    uppers = [upper_x, upper_y, above]
    flux = jnp.zeros_like(field)
    for direction in range(3):
        speed = velocity[direction][:, None, None]
        flux = flux + jnp.maximum(speed, 0.0) * (field - lowers[direction])
        flux = flux + jnp.minimum(speed, 0.0) * (uppers[direction] - field)
    return field - courant * flux


def with_halo(block, sides, width):
    for axis, dim in sides:
        count = lax.axis_size(axis)
        forward = [(i, i + 1) for i in range(count - 1)]
        backward = [(target, source) for source, target in forward]
        low = lax.ppermute(
            lax.slice_in_dim(block, block.shape[dim] - width, None, axis=dim), axis, forward
        )
        high = lax.ppermute(lax.slice_in_dim(block, 0, width, axis=dim), axis, backward)
        block = jnp.concatenate([low, block, high], axis=dim)
    return block


def gain_kernel(*refs, group, rows, pieces):
    t_refs = refs[:pieces]
    x_ref, xi_ref, o_ref = refs[pieces:]
    x = x_ref[...]
    tile = x.shape[-1]
    n_groups = o_ref.shape[1] // group

    def body(g, carry):
        start = pl.multiple_of(g * group * rows, group * rows)
        acc = None
        for p in range(pieces):
            t = t_refs[p][pl.ds(start, group * rows), :]
            inner = jnp.dot(t, x, preferred_element_type=jnp.float32)
            inner = inner.reshape(group, rows, tile)
            term = jnp.sum(inner * xi_ref[p].astype(jnp.float32)[None], axis=1)
            acc = term if acc is None else acc + term
        o_ref[0, pl.ds(pl.multiple_of(g * group, group), group), :] = acc
        return carry

    lax.fori_loop(0, n_groups, body, 0)


def contract(tensors, columns, factor, k_count, tile, group=8):
    kr, width = tensors[0].shape
    pieces = len(tensors)
    rows = kr // k_count
    total = columns.shape[1]
    kernel = functools.partial(gain_kernel, group=group, rows=rows, pieces=pieces)
    return pl.pallas_call(
        kernel,
        out_shape=jax.ShapeDtypeStruct((total // tile, k_count, tile), jnp.float32),
        grid=(total // tile,),
        in_specs=[pl.BlockSpec((kr, width), lambda c: (0, 0)) for _ in range(pieces)]
        + [
            pl.BlockSpec((width, tile), lambda c: (0, c)),
            pl.BlockSpec((pieces, rows, tile), lambda c: (0, 0, c)),
        ],
        out_specs=pl.BlockSpec((1, k_count, tile), lambda c: (c, 0, 0)),
        compiler_params=pltpu.CompilerParams(vmem_limit_bytes=48 * 1024 * 1024),
        cost_estimate=pl.CostEstimate(
            flops=2 * pieces * kr * width * total + 2 * pieces * kr * total,
            bytes_accessed=pieces * kr * width * 2 + width * total * 2 + pieces * rows * total * 2 + k_count * total * 4,
            transcendentals=0,
        ),
    )(*tensors, columns, factor)


def ring_pieces(x, axis):
    count = lax.axis_size(axis)
    return [x] + [
        lax.ppermute(x, axis, [(i, (i + d) % count) for i in range(count)]) for d in range(1, count)
    ]


def ring_sum_back(partial, axis):
    count = lax.axis_size(axis)
    total = partial[0]
    for d in range(1, count):
        total = total + lax.ppermute(partial[d], axis, [(i, (i - d) % count) for i in range(count)])
    return total


def swap_pair(x):
    return lax.ppermute(x, "mc", [(0, 1), (1, 0)])


def in_core_order(first_core, mine, other, axis):
    a = jnp.concatenate([mine, other], axis=axis)
    b = jnp.concatenate([other, mine], axis=axis)
    return jnp.where(first_core, a, b)


def per_device(density, tensor, velocity, inflow, flags):
    rows, depth, cells = density.shape
    position = lax.axis_index(SPACE)
    final = lax.axis_size(SPACE) - 1
    ghost_low = flags[0].astype(jnp.float32)[None, :] * inflow[:, None]
    ghost_high = flags[1].astype(jnp.float32)[None, :] * inflow[:, None]

    k_count, i_count, width = tensor.shape
    tensors = ring_pieces(tensor.reshape(k_count * i_count, width), "sy")

    field = density
    for substep in range(SUBSTEPS):
        padded = with_halo(field, ((SPACE, 1),), 1)
        low_plane = jnp.where(position == 0, ghost_low, padded[:, 0])
        high_plane = jnp.where(position == final, ghost_high, padded[:, -1])
        below = jnp.concatenate([low_plane[:, None], padded[:, 1:-2]], axis=1)
        above = jnp.concatenate([padded[:, 2:-1], high_plane[:, None]], axis=1)
        field = upwind(field, below, above, velocity)

    field, tensors = lax.optimization_barrier((field, tensors))
    coarse = field.astype(jnp.bfloat16)
    mode_count = lax.axis_size(MODE)
    copies = jnp.broadcast_to(coarse[None], (mode_count,) + coarse.shape)
    all_modes = lax.all_to_all(copies, MODE, 0, 0, tiled=True)
    all_modes = all_modes.reshape(mode_count * rows, depth * cells)
    modes = all_modes.shape[0]
    columns = jnp.concatenate(ring_pieces(all_modes, "sx"), axis=1)

    sx = lax.axis_index("sx")
    sy = lax.axis_index("sy")
    ny = lax.axis_size("sy")
    factor = jnp.stack(
        [
            lax.dynamic_slice_in_dim(
                columns, (sx * ny + (sy - d) % ny) * i_count, i_count, axis=0
            )
            for d in range(ny)
        ]
    )
    partial = contract(tensors, columns, factor, k_count, depth * cells)
    gain = ring_sum_back(partial, "sx")
    return field + time_step * gain.reshape(field.shape)


def solution(mesh):
    devices = mesh.devices
    space, mode = devices.shape
    fine = Mesh(devices.reshape(4, space // 4, mode // 2, 2), SPACE + MODE)
    in_specs = (P(MODE, SPACE, None), P(MODE, SPACE, None), P(None, MODE), P(MODE), P())
    out_specs = P(MODE, SPACE, None)
    return jax.shard_map(
        per_device, mesh=fine, in_specs=in_specs, out_specs=out_specs, check_vma=False
    )
```

```python
import functools

import jax
import jax.numpy as jnp
from jax import lax
from jax.experimental import pallas as pl
from jax.experimental.pallas import tpu as pltpu
from jax.sharding import Mesh
from jax.sharding import PartitionSpec as P

NXY = 16
SUBSTEPS = 3
HALO = SUBSTEPS

courant = 0.3
time_step = 0.5


SPACE = ("sx", "sy")
MODE = ("mz", "mc")


def neighbours(field):
    rows, planes, cells = field.shape
    grid = field.reshape(rows, planes, NXY, NXY)
    padded = jnp.pad(grid, ((0, 0), (0, 0), (1, 1), (1, 1)))
    lower_x = padded[:, :, :-2, 1:-1].reshape(field.shape)
    upper_x = padded[:, :, 2:, 1:-1].reshape(field.shape)
    lower_y = padded[:, :, 1:-1, :-2].reshape(field.shape)
    upper_y = padded[:, :, 1:-1, 2:].reshape(field.shape)
    return (lower_x, upper_x, lower_y, upper_y)


def upwind(field, below, above, velocity):
    lower_x, upper_x, lower_y, upper_y = neighbours(field)
    lowers = [lower_x, lower_y, below]
    uppers = [upper_x, upper_y, above]
    flux = jnp.zeros_like(field)
    for direction in range(3):
        speed = velocity[direction][:, None, None]
        flux = flux + jnp.maximum(speed, 0.0) * (field - lowers[direction])
        flux = flux + jnp.minimum(speed, 0.0) * (uppers[direction] - field)
    return field - courant * flux


def with_halo(block, sides, width):
    for axis, dim in sides:
        count = lax.axis_size(axis)
        forward = [(i, i + 1) for i in range(count - 1)]
        backward = [(target, source) for source, target in forward]
        low = lax.ppermute(
            lax.slice_in_dim(block, block.shape[dim] - width, None, axis=dim), axis, forward
        )
        high = lax.ppermute(lax.slice_in_dim(block, 0, width, axis=dim), axis, backward)
        block = jnp.concatenate([low, block, high], axis=dim)
    return block


def gain_kernel(t_ref, x_ref, xi_ref, o_ref, *, group, rows):
    x = x_ref[...]
    xi = xi_ref[...].astype(jnp.float32)
    pieces, k_count, cells = o_ref.shape
    n_groups = k_count // group

    def body(g, carry):
        start = pl.multiple_of(g * group * rows, group * rows)
        t = t_ref[pl.ds(start, group * rows), :]
        inner = jnp.dot(t, x, preferred_element_type=jnp.float32)
        inner = inner.reshape(group, rows, inner.shape[-1])
        out = jnp.sum(inner * xi[None], axis=1)
        for p in range(pieces):
            o_ref[p, pl.ds(pl.multiple_of(g * group, group), group), :] = out[:, p * cells : (p + 1) * cells]
        return carry

    lax.fori_loop(0, n_groups, body, 0)


def contract(tensor2d, columns, factor, k_count, cells, tile=512, group=8):
    kr, width = tensor2d.shape
    rows = kr // k_count
    total = columns.shape[1]
    kernel = functools.partial(gain_kernel, group=group, rows=rows)
    return pl.pallas_call(
        kernel,
        out_shape=jax.ShapeDtypeStruct((total // cells, k_count, cells), jnp.float32),
        grid=(total // tile,),
        in_specs=[
            pl.BlockSpec((kr, width), lambda c: (0, 0)),
            pl.BlockSpec((width, tile), lambda c: (0, c)),
            pl.BlockSpec((rows, tile), lambda c: (0, c)),
        ],
        out_specs=pl.BlockSpec((tile // cells, k_count, cells), lambda c: (c, 0, 0)),
        compiler_params=pltpu.CompilerParams(vmem_limit_bytes=48 * 1024 * 1024),
        cost_estimate=pl.CostEstimate(
            flops=2 * kr * width * total + 2 * kr * total,
            bytes_accessed=kr * width * 2 + width * total * 2 + rows * total * 2 + k_count * total * 4,
            transcendentals=0,
        ),
    )(tensor2d, columns, factor)


def ring_gather(x, axis):
    count = lax.axis_size(axis)
    me = lax.axis_index(axis)
    pieces = [x]
    for d in range(1, count):
        pieces.append(lax.ppermute(x, axis, [(i, (i + d) % count) for i in range(count)]))
    stacked = jnp.stack(pieces[::-1], axis=0)
    return jnp.roll(stacked, me + 1, axis=0)


def ring_reduce_scatter(pieces, axis):
    count = lax.axis_size(axis)
    me = lax.axis_index(axis)
    total = lax.dynamic_index_in_dim(pieces, me, axis=0, keepdims=False)
    for d in range(1, count):
        piece = lax.dynamic_index_in_dim(pieces, (me + d) % count, axis=0, keepdims=False)
        total = total + lax.ppermute(piece, axis, [(i, (i + d) % count) for i in range(count)])
    return total


def swap_pair(x):
    return lax.ppermute(x, "mc", [(0, 1), (1, 0)])


def in_core_order(first_core, mine, other, axis):
    a = jnp.concatenate([mine, other], axis=axis)
    b = jnp.concatenate([other, mine], axis=axis)
    return jnp.where(first_core, a, b)


def per_device(density, tensor, velocity, inflow, flags):
    rows, depth, cells = density.shape
    position = lax.axis_index(SPACE)
    final = lax.axis_size(SPACE) - 1
    ghost_low = flags[0].astype(jnp.float32)[None, :] * inflow[:, None]
    ghost_high = flags[1].astype(jnp.float32)[None, :] * inflow[:, None]

    with jax.named_scope("tgather"):
        wide_tensor = lax.all_gather(tensor, "sy", axis=1, tiled=True)

    field = density
    for substep in range(SUBSTEPS):
        with jax.named_scope(f"substep{substep}"):
            padded = with_halo(field, ((SPACE, 1),), 1)
            low_plane = jnp.where(position == 0, ghost_low, padded[:, 0])
            high_plane = jnp.where(position == final, ghost_high, padded[:, -1])
            below = jnp.concatenate([low_plane[:, None], padded[:, 1:-2]], axis=1)
            above = jnp.concatenate([padded[:, 2:-1], high_plane[:, None]], axis=1)
            field = upwind(field, below, above, velocity)

    coarse = field.astype(jnp.bfloat16)
    all_modes = lax.all_gather(coarse, MODE, axis=0, tiled=True)
    all_modes, wide_tensor = lax.optimization_barrier((all_modes, wide_tensor))
    columns = lax.all_gather(all_modes, "sx", axis=1, tiled=True)
    modes = columns.shape[0]
    columns = columns.reshape(modes, -1)

    k_count, i_count, width = wide_tensor.shape
    sx = lax.axis_index("sx")
    factor = lax.dynamic_slice_in_dim(columns, sx * i_count, i_count, axis=0)
    partial = contract(
        wide_tensor.reshape(k_count * i_count, width), columns, factor, k_count, depth * cells
    )
    gain = ring_reduce_scatter(partial, "sx")
    return field + time_step * gain.reshape(field.shape)


def solution(mesh):
    devices = mesh.devices
    space, mode = devices.shape
    fine = Mesh(devices.reshape(4, space // 4, mode // 2, 2), SPACE + MODE)
    in_specs = (P(MODE, SPACE, None), P(MODE, SPACE, None), P(None, MODE), P(MODE), P())
    out_specs = P(MODE, SPACE, None)
    return jax.shard_map(
        per_device, mesh=fine, in_specs=in_specs, out_specs=out_specs, check_vma=False
    )
```

```python
import functools

import jax
import jax.numpy as jnp
from jax import lax
from jax.experimental import pallas as pl
from jax.experimental.pallas import tpu as pltpu
from jax.sharding import Mesh
from jax.sharding import PartitionSpec as P

NXY = 16
SUBSTEPS = 3
HALO = SUBSTEPS

courant = 0.3
time_step = 0.5


SPACE = ("sx", "sy")
MODE = ("mz", "mc")


def neighbours(field):
    rows, planes, cells = field.shape
    grid = field.reshape(rows, planes, NXY, NXY)
    padded = jnp.pad(grid, ((0, 0), (0, 0), (1, 1), (1, 1)))
    lower_x = padded[:, :, :-2, 1:-1].reshape(field.shape)
    upper_x = padded[:, :, 2:, 1:-1].reshape(field.shape)
    lower_y = padded[:, :, 1:-1, :-2].reshape(field.shape)
    upper_y = padded[:, :, 1:-1, 2:].reshape(field.shape)
    return (lower_x, upper_x, lower_y, upper_y)


def upwind(field, below, above, velocity):
    lower_x, upper_x, lower_y, upper_y = neighbours(field)
    lowers = [lower_x, lower_y, below]
    uppers = [upper_x, upper_y, above]
    flux = jnp.zeros_like(field)
    for direction in range(3):
        speed = velocity[direction][:, None, None]
        flux = flux + jnp.maximum(speed, 0.0) * (field - lowers[direction])
        flux = flux + jnp.minimum(speed, 0.0) * (uppers[direction] - field)
    return field - courant * flux


def with_halo(block, sides, width):
    for axis, dim in sides:
        count = lax.axis_size(axis)
        forward = [(i, i + 1) for i in range(count - 1)]
        backward = [(target, source) for source, target in forward]
        low = lax.ppermute(
            lax.slice_in_dim(block, block.shape[dim] - width, None, axis=dim), axis, forward
        )
        high = lax.ppermute(lax.slice_in_dim(block, 0, width, axis=dim), axis, backward)
        block = jnp.concatenate([low, block, high], axis=dim)
    return block


def plane_step(f, lower_z, upper_z, vel, x_lo, x_hi, y_lo, y_hi):
    cells = f.shape[-1]
    zero = jnp.zeros_like(f)
    lower_x = jnp.where(x_lo, zero, pltpu.roll(f, NXY, 1))
    upper_x = jnp.where(x_hi, zero, pltpu.roll(f, cells - NXY, 1))
    lower_y = jnp.where(y_lo, zero, pltpu.roll(f, 1, 1))
    upper_y = jnp.where(y_hi, zero, pltpu.roll(f, cells - 1, 1))
    lowers = [lower_x, lower_y, lower_z]
    uppers = [upper_x, upper_y, upper_z]
    flux = jnp.zeros_like(f)
    for direction in range(3):
        speed = vel[direction]
        flux = flux + jnp.maximum(speed, 0.0) * (f - lowers[direction])
        flux = flux + jnp.minimum(speed, 0.0) * (uppers[direction] - f)
    return f - courant * flux


def transport_kernel(pos_ref, b2_ref, b1_ref, d_ref, a1_ref, a2_ref, v_ref, gl_ref, gh_ref, o_ref, *, total_planes):
    depth = d_ref.shape[1]
    halo = SUBSTEPS
    extra = halo - depth
    planes = [b2_ref[:, depth - extra + i, :] for i in range(extra)]
    planes += [b1_ref[:, p, :] for p in range(depth)]
    planes += [d_ref[:, p, :] for p in range(depth)]
    planes += [a1_ref[:, p, :] for p in range(depth)]
    planes += [a2_ref[:, i, :] for i in range(extra)]
    rows, cells = planes[0].shape
    pos = pos_ref[0]
    gl = gl_ref[...]
    gh = gh_ref[...]
    vel = [v_ref[d] for d in range(3)]
    lane = lax.broadcasted_iota(jnp.int32, (rows, cells), 1)
    y = lane % NXY
    x = lane // NXY
    x_lo, x_hi, y_lo, y_hi = x == 0, x == NXY - 1, y == 0, y == NXY - 1

    def fix(e, f):
        z = pos * depth - halo + e
        f = jnp.where(z < 0, gl, f)
        return jnp.where(z >= total_planes, gh, f)

    field = [fix(e, f) for e, f in enumerate(planes)]
    n = len(field)
    for t in range(1, SUBSTEPS + 1):
        new = [None] * n
        for e in range(t, n - t):
            new[e] = fix(e, plane_step(field[e], field[e - 1], field[e + 1], vel, x_lo, x_hi, y_lo, y_hi))
        field = new
    for p in range(depth):
        o_ref[:, p, :] = field[halo + p]


def run_transport(pos, b2, b1, d, a1, a2, vel3, gl, gh, total_planes):
    rows, depth, cells = d.shape
    vmem = pltpu.VMEM
    spec = pl.BlockSpec(memory_space=vmem)
    return pl.pallas_call(
        functools.partial(transport_kernel, total_planes=total_planes),
        out_shape=jax.ShapeDtypeStruct(d.shape, d.dtype),
        in_specs=[pl.BlockSpec(memory_space=pltpu.SMEM)] + [spec] * 8,
        out_specs=spec,
    )(pos, b2, b1, d, a1, a2, vel3, gl, gh)


def gain_kernel(t_ref, x_ref, xi_ref, o_ref, *, group, rows):
    x = x_ref[...]
    xi = xi_ref[...].astype(jnp.float32)
    pieces, k_count, cells = o_ref.shape
    n_groups = k_count // group

    def body(g, carry):
        start = pl.multiple_of(g * group * rows, group * rows)
        t = t_ref[pl.ds(start, group * rows), :]
        inner = jnp.dot(t, x, preferred_element_type=jnp.float32)
        inner = inner.reshape(group, rows, inner.shape[-1])
        out = jnp.sum(inner * xi[None], axis=1)
        for p in range(pieces):
            o_ref[p, pl.ds(pl.multiple_of(g * group, group), group), :] = out[:, p * cells : (p + 1) * cells]
        return carry

    lax.fori_loop(0, n_groups, body, 0)


def contract(tensor2d, columns, factor, k_count, cells, tile=512, group=8):
    kr, width = tensor2d.shape
    rows = kr // k_count
    total = columns.shape[1]
    kernel = functools.partial(gain_kernel, group=group, rows=rows)
    return pl.pallas_call(
        kernel,
        out_shape=jax.ShapeDtypeStruct((total // cells, k_count, cells), jnp.float32),
        grid=(total // tile,),
        in_specs=[
            pl.BlockSpec((kr, width), lambda c: (0, 0)),
            pl.BlockSpec((width, tile), lambda c: (0, c)),
            pl.BlockSpec((rows, tile), lambda c: (0, c)),
        ],
        out_specs=pl.BlockSpec((tile // cells, k_count, cells), lambda c: (c, 0, 0)),
        compiler_params=pltpu.CompilerParams(vmem_limit_bytes=48 * 1024 * 1024),
        cost_estimate=pl.CostEstimate(
            flops=2 * kr * width * total + 2 * kr * total,
            bytes_accessed=kr * width * 2 + width * total * 2 + rows * total * 2 + k_count * total * 4,
            transcendentals=0,
        ),
    )(tensor2d, columns, factor)


def ring_gather(x, axis):
    count = lax.axis_size(axis)
    me = lax.axis_index(axis)
    pieces = [x]
    for d in range(1, count):
        pieces.append(lax.ppermute(x, axis, [(i, (i + d) % count) for i in range(count)]))
    stacked = jnp.stack(pieces[::-1], axis=0)
    return jnp.roll(stacked, me + 1, axis=0)


def ring_reduce_scatter(pieces, axis):
    count = lax.axis_size(axis)
    me = lax.axis_index(axis)
    total = lax.dynamic_index_in_dim(pieces, me, axis=0, keepdims=False)
    for d in range(1, count):
        piece = lax.dynamic_index_in_dim(pieces, (me + d) % count, axis=0, keepdims=False)
        total = total + lax.ppermute(piece, axis, [(i, (i + d) % count) for i in range(count)])
    return total


def swap_pair(x):
    return lax.ppermute(x, "mc", [(0, 1), (1, 0)])


def in_core_order(first_core, mine, other, axis):
    a = jnp.concatenate([mine, other], axis=axis)
    b = jnp.concatenate([other, mine], axis=axis)
    return jnp.where(first_core, a, b)


def per_device(density, tensor, velocity, inflow, flags):
    rows, depth, cells = density.shape
    position = lax.axis_index(SPACE)
    final = lax.axis_size(SPACE) - 1
    ghost_low = flags[0].astype(jnp.float32)[None, :] * inflow[:, None]
    ghost_high = flags[1].astype(jnp.float32)[None, :] * inflow[:, None]

    with jax.named_scope("tgather"):
        wide_tensor = lax.all_gather(tensor, "sy", axis=1, tiled=True)

    count = lax.axis_size(SPACE)
    halo_from = lambda d: lax.ppermute(
        density, SPACE, [(i, i + d) for i in range(max(0, -d), min(count, count - d))]
    )
    field = run_transport(
        position.reshape(1).astype(jnp.int32),
        halo_from(2),
        halo_from(1),
        density,
        halo_from(-1),
        halo_from(-2),
        velocity[:, :, None],
        ghost_low,
        ghost_high,
        count * depth,
    )

    coarse = field.astype(jnp.bfloat16)
    all_modes = lax.all_gather(coarse, MODE, axis=0, tiled=True)
    all_modes, wide_tensor = lax.optimization_barrier((all_modes, wide_tensor))
    columns = lax.all_gather(all_modes, "sx", axis=1, tiled=True)
    modes = columns.shape[0]
    columns = columns.reshape(modes, -1)

    k_count, i_count, width = wide_tensor.shape
    sx = lax.axis_index("sx")
    factor = lax.dynamic_slice_in_dim(columns, sx * i_count, i_count, axis=0)
    partial = contract(
        wide_tensor.reshape(k_count * i_count, width), columns, factor, k_count, depth * cells
    )
    gain = ring_reduce_scatter(partial, "sx")
    return field + time_step * gain.reshape(field.shape)


def solution(mesh):
    devices = mesh.devices
    space, mode = devices.shape
    fine = Mesh(devices.reshape(4, space // 4, mode // 2, 2), SPACE + MODE)
    in_specs = (P(MODE, SPACE, None), P(MODE, SPACE, None), P(None, MODE), P(MODE), P())
    out_specs = P(MODE, SPACE, None)
    return jax.shard_map(
        per_device, mesh=fine, in_specs=in_specs, out_specs=out_specs, check_vma=False
    )
```

```python
import functools

import jax
import jax.numpy as jnp
from jax import lax
from jax.experimental import pallas as pl
from jax.experimental.pallas import tpu as pltpu
from jax.sharding import Mesh
from jax.sharding import PartitionSpec as P

NXY = 16
SUBSTEPS = 3
HALO = SUBSTEPS

courant = 0.3
time_step = 0.5


SPACE = ("sx", "sy")
MODE = ("mz", "mc")


def neighbours(field):
    rows, planes, cells = field.shape
    grid = field.reshape(rows, planes, NXY, NXY)
    padded = jnp.pad(grid, ((0, 0), (0, 0), (1, 1), (1, 1)))
    lower_x = padded[:, :, :-2, 1:-1].reshape(field.shape)
    upper_x = padded[:, :, 2:, 1:-1].reshape(field.shape)
    lower_y = padded[:, :, 1:-1, :-2].reshape(field.shape)
    upper_y = padded[:, :, 1:-1, 2:].reshape(field.shape)
    return (lower_x, upper_x, lower_y, upper_y)


def upwind(field, below, above, velocity):
    lower_x, upper_x, lower_y, upper_y = neighbours(field)
    lowers = [lower_x, lower_y, below]
    uppers = [upper_x, upper_y, above]
    flux = jnp.zeros_like(field)
    for direction in range(3):
        speed = velocity[direction][:, None, None]
        flux = flux + jnp.maximum(speed, 0.0) * (field - lowers[direction])
        flux = flux + jnp.minimum(speed, 0.0) * (uppers[direction] - field)
    return field - courant * flux


def with_halo(block, sides, width):
    for axis, dim in sides:
        count = lax.axis_size(axis)
        forward = [(i, i + 1) for i in range(count - 1)]
        backward = [(target, source) for source, target in forward]
        low = lax.ppermute(
            lax.slice_in_dim(block, block.shape[dim] - width, None, axis=dim), axis, forward
        )
        high = lax.ppermute(lax.slice_in_dim(block, 0, width, axis=dim), axis, backward)
        block = jnp.concatenate([low, block, high], axis=dim)
    return block


def plane_step(f, lower_z, upper_z, vel, x_lo, x_hi, y_lo, y_hi):
    cells = f.shape[-1]
    zero = jnp.zeros_like(f)
    lower_x = jnp.where(x_lo, zero, pltpu.roll(f, NXY, 1))
    upper_x = jnp.where(x_hi, zero, pltpu.roll(f, cells - NXY, 1))
    lower_y = jnp.where(y_lo, zero, pltpu.roll(f, 1, 1))
    upper_y = jnp.where(y_hi, zero, pltpu.roll(f, cells - 1, 1))
    lowers = [lower_x, lower_y, lower_z]
    uppers = [upper_x, upper_y, upper_z]
    flux = jnp.zeros_like(f)
    for direction in range(3):
        speed = vel[direction]
        flux = flux + jnp.maximum(speed, 0.0) * (f - lowers[direction])
        flux = flux + jnp.minimum(speed, 0.0) * (uppers[direction] - f)
    return f - courant * flux


def transport_kernel(pos_ref, b2_ref, b1_ref, d_ref, a1_ref, a2_ref, v_ref, gl_ref, gh_ref, o_ref, *, total_planes):
    depth = d_ref.shape[1]
    halo = SUBSTEPS
    extra = halo - depth
    planes = [b2_ref[:, depth - extra + i, :] for i in range(extra)]
    planes += [b1_ref[:, p, :] for p in range(depth)]
    planes += [d_ref[:, p, :] for p in range(depth)]
    planes += [a1_ref[:, p, :] for p in range(depth)]
    planes += [a2_ref[:, i, :] for i in range(extra)]
    rows, cells = planes[0].shape
    pos = pos_ref[0]
    gl = gl_ref[...]
    gh = gh_ref[...]
    vel = [v_ref[d] for d in range(3)]
    lane = lax.broadcasted_iota(jnp.int32, (rows, cells), 1)
    y = lane % NXY
    x = lane // NXY
    x_lo, x_hi, y_lo, y_hi = x == 0, x == NXY - 1, y == 0, y == NXY - 1

    def fix(e, f):
        z = pos * depth - halo + e
        f = jnp.where(z < 0, gl, f)
        return jnp.where(z >= total_planes, gh, f)

    field = [fix(e, f) for e, f in enumerate(planes)]
    n = len(field)
    for t in range(1, SUBSTEPS + 1):
        new = [None] * n
        for e in range(t, n - t):
            new[e] = fix(e, plane_step(field[e], field[e - 1], field[e + 1], vel, x_lo, x_hi, y_lo, y_hi))
        field = new
    for p in range(depth):
        o_ref[:, p, :] = field[halo + p]


def run_transport(pos, b2, b1, d, a1, a2, vel3, gl, gh, total_planes):
    rows, depth, cells = d.shape
    vmem = pltpu.VMEM
    spec = pl.BlockSpec(memory_space=vmem)
    return pl.pallas_call(
        functools.partial(transport_kernel, total_planes=total_planes),
        out_shape=jax.ShapeDtypeStruct(d.shape, d.dtype),
        in_specs=[pl.BlockSpec(memory_space=pltpu.SMEM)] + [spec] * 8,
        out_specs=spec,
    )(pos, b2, b1, d, a1, a2, vel3, gl, gh)


def gain_kernel(t_ref, x_ref, xi_ref, o_ref, *, group, rows):
    x = x_ref[...]
    xi = xi_ref[...].astype(jnp.float32)
    pieces, k_count, cells = o_ref.shape
    n_groups = k_count // group

    def body(g, carry):
        start = pl.multiple_of(g * group * rows, group * rows)
        t = t_ref[pl.ds(start, group * rows), :]
        inner = jnp.dot(t, x, preferred_element_type=jnp.float32)
        inner = inner.reshape(group, rows, inner.shape[-1])
        out = jnp.sum(inner * xi[None], axis=1)
        for p in range(pieces):
            o_ref[p, pl.ds(pl.multiple_of(g * group, group), group), :] = out[:, p * cells : (p + 1) * cells]
        return carry

    lax.fori_loop(0, n_groups, body, 0)


def contract(tensor2d, columns, factor, k_count, cells, tile=512, group=8):
    kr, width = tensor2d.shape
    rows = kr // k_count
    total = columns.shape[1]
    kernel = functools.partial(gain_kernel, group=group, rows=rows)
    return pl.pallas_call(
        kernel,
        out_shape=jax.ShapeDtypeStruct((total // cells, k_count, cells), jnp.float32),
        grid=(total // tile,),
        in_specs=[
            pl.BlockSpec((kr, width), lambda c: (0, 0)),
            pl.BlockSpec((width, tile), lambda c: (0, c)),
            pl.BlockSpec((rows, tile), lambda c: (0, c)),
        ],
        out_specs=pl.BlockSpec((tile // cells, k_count, cells), lambda c: (c, 0, 0)),
        compiler_params=pltpu.CompilerParams(vmem_limit_bytes=48 * 1024 * 1024),
        cost_estimate=pl.CostEstimate(
            flops=2 * kr * width * total + 2 * kr * total,
            bytes_accessed=kr * width * 2 + width * total * 2 + rows * total * 2 + k_count * total * 4,
            transcendentals=0,
        ),
    )(tensor2d, columns, factor)


def ring_gather(x, axis):
    count = lax.axis_size(axis)
    me = lax.axis_index(axis)
    pieces = [x]
    for d in range(1, count):
        pieces.append(lax.ppermute(x, axis, [(i, (i + d) % count) for i in range(count)]))
    stacked = jnp.stack(pieces[::-1], axis=0)
    return jnp.roll(stacked, me + 1, axis=0)


def ring_reduce_scatter(pieces, axis):
    count = lax.axis_size(axis)
    me = lax.axis_index(axis)
    total = lax.dynamic_index_in_dim(pieces, me, axis=0, keepdims=False)
    for d in range(1, count):
        piece = lax.dynamic_index_in_dim(pieces, (me + d) % count, axis=0, keepdims=False)
        total = total + lax.ppermute(piece, axis, [(i, (i + d) % count) for i in range(count)])
    return total


def ring_pieces(x, axis):
    count = lax.axis_size(axis)
    return [x] + [
        lax.ppermute(x, axis, [(i, (i + d) % count) for i in range(count)]) for d in range(1, count)
    ]


def ring_sum_back(partial, axis):
    count = lax.axis_size(axis)
    total = partial[0]
    for d in range(1, count):
        total = total + lax.ppermute(partial[d], axis, [(i, (i - d) % count) for i in range(count)])
    return total


def swap_pair(x):
    return lax.ppermute(x, "mc", [(0, 1), (1, 0)])


def in_core_order(first_core, mine, other, axis):
    a = jnp.concatenate([mine, other], axis=axis)
    b = jnp.concatenate([other, mine], axis=axis)
    return jnp.where(first_core, a, b)


def per_device(density, tensor, velocity, inflow, flags):
    rows, depth, cells = density.shape
    position = lax.axis_index(SPACE)
    final = lax.axis_size(SPACE) - 1
    ghost_low = flags[0].astype(jnp.float32)[None, :] * inflow[:, None]
    ghost_high = flags[1].astype(jnp.float32)[None, :] * inflow[:, None]

    with jax.named_scope("tgather"):
        wide_tensor = lax.all_gather(tensor, "sy", axis=1, tiled=True)

    count = lax.axis_size(SPACE)
    halo_from = lambda d: lax.ppermute(
        density, SPACE, [(i, i + d) for i in range(max(0, -d), min(count, count - d))]
    )
    field = run_transport(
        position.reshape(1).astype(jnp.int32),
        halo_from(2),
        halo_from(1),
        density,
        halo_from(-1),
        halo_from(-2),
        velocity[:, :, None],
        ghost_low,
        ghost_high,
        count * depth,
    )

    coarse = field.astype(jnp.bfloat16)
    all_modes = lax.all_gather(coarse, MODE, axis=0, tiled=True)
    modes = all_modes.shape[0]
    pieces = ring_pieces(all_modes.reshape(modes, -1), "sx")
    pieces, wide_tensor = lax.optimization_barrier((pieces, wide_tensor))
    columns = jnp.concatenate(pieces, axis=1)

    k_count, i_count, width = wide_tensor.shape
    sx = lax.axis_index("sx")
    factor = lax.dynamic_slice_in_dim(columns, sx * i_count, i_count, axis=0)
    partial = contract(
        wide_tensor.reshape(k_count * i_count, width), columns, factor, k_count, depth * cells
    )
    gain = ring_sum_back(partial, "sx")
    return field + time_step * gain.reshape(field.shape)


def solution(mesh):
    devices = mesh.devices
    space, mode = devices.shape
    fine = Mesh(devices.reshape(4, space // 4, mode // 2, 2), SPACE + MODE)
    in_specs = (P(MODE, SPACE, None), P(MODE, SPACE, None), P(None, MODE), P(MODE), P())
    out_specs = P(MODE, SPACE, None)
    return jax.shard_map(
        per_device, mesh=fine, in_specs=in_specs, out_specs=out_specs, check_vma=False
    )
```

```python
import functools

import jax
import jax.numpy as jnp
from jax import lax
from jax.experimental import pallas as pl
from jax.experimental.pallas import tpu as pltpu
from jax.sharding import Mesh
from jax.sharding import PartitionSpec as P

NXY = 16
SUBSTEPS = 3
HALO = SUBSTEPS

courant = 0.3
time_step = 0.5


SPACE = ("sx", "sy")
MODE = ("mz", "mc")


def neighbours(field):
    rows, planes, cells = field.shape
    grid = field.reshape(rows, planes, NXY, NXY)
    padded = jnp.pad(grid, ((0, 0), (0, 0), (1, 1), (1, 1)))
    lower_x = padded[:, :, :-2, 1:-1].reshape(field.shape)
    upper_x = padded[:, :, 2:, 1:-1].reshape(field.shape)
    lower_y = padded[:, :, 1:-1, :-2].reshape(field.shape)
    upper_y = padded[:, :, 1:-1, 2:].reshape(field.shape)
    return (lower_x, upper_x, lower_y, upper_y)


def upwind(field, below, above, velocity):
    lower_x, upper_x, lower_y, upper_y = neighbours(field)
    lowers = [lower_x, lower_y, below]
    uppers = [upper_x, upper_y, above]
    flux = jnp.zeros_like(field)
    for direction in range(3):
        speed = velocity[direction][:, None, None]
        flux = flux + jnp.maximum(speed, 0.0) * (field - lowers[direction])
        flux = flux + jnp.minimum(speed, 0.0) * (uppers[direction] - field)
    return field - courant * flux


def with_halo(block, sides, width):
    for axis, dim in sides:
        count = lax.axis_size(axis)
        forward = [(i, i + 1) for i in range(count - 1)]
        backward = [(target, source) for source, target in forward]
        low = lax.ppermute(
            lax.slice_in_dim(block, block.shape[dim] - width, None, axis=dim), axis, forward
        )
        high = lax.ppermute(lax.slice_in_dim(block, 0, width, axis=dim), axis, backward)
        block = jnp.concatenate([low, block, high], axis=dim)
    return block


def plane_step(f, lower_z, upper_z, vel, x_lo, x_hi, y_lo, y_hi):
    cells = f.shape[-1]
    zero = jnp.zeros_like(f)
    lower_x = jnp.where(x_lo, zero, pltpu.roll(f, NXY, 1))
    upper_x = jnp.where(x_hi, zero, pltpu.roll(f, cells - NXY, 1))
    lower_y = jnp.where(y_lo, zero, pltpu.roll(f, 1, 1))
    upper_y = jnp.where(y_hi, zero, pltpu.roll(f, cells - 1, 1))
    lowers = [lower_x, lower_y, lower_z]
    uppers = [upper_x, upper_y, upper_z]
    flux = jnp.zeros_like(f)
    for direction in range(3):
        speed = vel[direction]
        flux = flux + jnp.maximum(speed, 0.0) * (f - lowers[direction])
        flux = flux + jnp.minimum(speed, 0.0) * (uppers[direction] - f)
    return f - courant * flux


def transport_kernel(pos_ref, b2_ref, b1_ref, d_ref, a1_ref, a2_ref, v_ref, gl_ref, gh_ref, o_ref, *, total_planes):
    depth = d_ref.shape[1]
    halo = SUBSTEPS
    extra = halo - depth
    planes = [b2_ref[:, depth - extra + i, :] for i in range(extra)]
    planes += [b1_ref[:, p, :] for p in range(depth)]
    planes += [d_ref[:, p, :] for p in range(depth)]
    planes += [a1_ref[:, p, :] for p in range(depth)]
    planes += [a2_ref[:, i, :] for i in range(extra)]
    rows, cells = planes[0].shape
    pos = pos_ref[0]
    gl = gl_ref[...]
    gh = gh_ref[...]
    vel = [v_ref[d] for d in range(3)]
    lane = lax.broadcasted_iota(jnp.int32, (rows, cells), 1)
    y = lane % NXY
    x = lane // NXY
    x_lo, x_hi, y_lo, y_hi = x == 0, x == NXY - 1, y == 0, y == NXY - 1

    def fix(e, f):
        z = pos * depth - halo + e
        f = jnp.where(z < 0, gl, f)
        return jnp.where(z >= total_planes, gh, f)

    field = [fix(e, f) for e, f in enumerate(planes)]
    n = len(field)
    for t in range(1, SUBSTEPS + 1):
        new = [None] * n
        for e in range(t, n - t):
            new[e] = fix(e, plane_step(field[e], field[e - 1], field[e + 1], vel, x_lo, x_hi, y_lo, y_hi))
        field = new
    for p in range(depth):
        o_ref[:, p, :] = field[halo + p]


def run_transport(pos, b2, b1, d, a1, a2, vel3, gl, gh, total_planes):
    rows, depth, cells = d.shape
    vmem = pltpu.VMEM
    spec = pl.BlockSpec(memory_space=vmem)
    return pl.pallas_call(
        functools.partial(transport_kernel, total_planes=total_planes),
        out_shape=jax.ShapeDtypeStruct(d.shape, d.dtype),
        in_specs=[pl.BlockSpec(memory_space=pltpu.SMEM)] + [spec] * 8,
        out_specs=spec,
    )(pos, b2, b1, d, a1, a2, vel3, gl, gh)


def gain_kernel(*refs, group, rows, pieces):
    t_refs = refs[:pieces]
    x_ref, xi_ref, o_ref = refs[pieces:]
    x = x_ref[...]
    tile = x.shape[-1]
    n_groups = o_ref.shape[1] // group

    def body(g, carry):
        start = pl.multiple_of(g * group * rows, group * rows)
        acc = None
        for p in range(pieces):
            t = t_refs[p][pl.ds(start, group * rows), :]
            inner = jnp.dot(t, x, preferred_element_type=jnp.float32)
            inner = inner.reshape(group, rows, tile)
            term = jnp.sum(inner * xi_ref[p].astype(jnp.float32)[None], axis=1)
            acc = term if acc is None else acc + term
        o_ref[0, pl.ds(pl.multiple_of(g * group, group), group), :] = acc
        return carry

    lax.fori_loop(0, n_groups, body, 0)


def contract(tensors, columns, factor, k_count, tile, group=8):
    kr, width = tensors[0].shape
    pieces = len(tensors)
    rows = kr // k_count
    total = columns.shape[1]
    kernel = functools.partial(gain_kernel, group=group, rows=rows, pieces=pieces)
    return pl.pallas_call(
        kernel,
        out_shape=jax.ShapeDtypeStruct((total // tile, k_count, tile), jnp.float32),
        grid=(total // tile,),
        in_specs=[pl.BlockSpec((kr, width), lambda c: (0, 0)) for _ in range(pieces)]
        + [
            pl.BlockSpec((width, tile), lambda c: (0, c)),
            pl.BlockSpec((pieces, rows, tile), lambda c: (0, 0, c)),
        ],
        out_specs=pl.BlockSpec((1, k_count, tile), lambda c: (c, 0, 0)),
        compiler_params=pltpu.CompilerParams(vmem_limit_bytes=48 * 1024 * 1024),
        cost_estimate=pl.CostEstimate(
            flops=2 * pieces * kr * width * total + 2 * pieces * kr * total,
            bytes_accessed=pieces * kr * width * 2 + width * total * 2 + pieces * rows * total * 2 + k_count * total * 4,
            transcendentals=0,
        ),
    )(*tensors, columns, factor)


def ring_pieces(x, axis):
    count = lax.axis_size(axis)
    return [x] + [
        lax.ppermute(x, axis, [(i, (i + d) % count) for i in range(count)]) for d in range(1, count)
    ]


def ring_sum_back(partial, axis):
    count = lax.axis_size(axis)
    total = partial[0]
    for d in range(1, count):
        total = total + lax.ppermute(partial[d], axis, [(i, (i - d) % count) for i in range(count)])
    return total


def swap_pair(x):
    return lax.ppermute(x, "mc", [(0, 1), (1, 0)])


def in_core_order(first_core, mine, other, axis):
    a = jnp.concatenate([mine, other], axis=axis)
    b = jnp.concatenate([other, mine], axis=axis)
    return jnp.where(first_core, a, b)


def per_device(density, tensor, velocity, inflow, flags):
    rows, depth, cells = density.shape
    position = lax.axis_index(SPACE)
    final = lax.axis_size(SPACE) - 1
    ghost_low = flags[0].astype(jnp.float32)[None, :] * inflow[:, None]
    ghost_high = flags[1].astype(jnp.float32)[None, :] * inflow[:, None]

    count = lax.axis_size(SPACE)
    halo_from = lambda d: lax.ppermute(
        density, SPACE, [(i, i + d) for i in range(max(0, -d), min(count, count - d))]
    )
    halos = [halo_from(2), halo_from(1), halo_from(-1), halo_from(-2)]
    halos, tensor = lax.optimization_barrier((halos, tensor))
    k_count, i_count, width = tensor.shape
    tensors = ring_pieces(tensor.reshape(k_count * i_count, width), "sy")
    field = run_transport(
        position.reshape(1).astype(jnp.int32),
        halos[0],
        halos[1],
        density,
        halos[2],
        halos[3],
        velocity[:, :, None],
        ghost_low,
        ghost_high,
        count * depth,
    )

    coarse = field.astype(jnp.bfloat16)
    all_modes = lax.all_gather(coarse, MODE, axis=0, tiled=True)
    modes = all_modes.shape[0]
    pieces = ring_pieces(all_modes.reshape(modes, -1), "sx")
    pieces, tensors = lax.optimization_barrier((pieces, tensors))
    columns = jnp.concatenate(pieces, axis=1)

    sx = lax.axis_index("sx")
    sy = lax.axis_index("sy")
    ny = lax.axis_size("sy")
    factor = jnp.stack(
        [
            lax.dynamic_slice_in_dim(
                columns, (sx * ny + (sy - d) % ny) * i_count, i_count, axis=0
            )
            for d in range(ny)
        ]
    )
    partial = contract(tensors, columns, factor, k_count, depth * cells)
    gain = ring_sum_back(partial, "sx")
    return field + time_step * gain.reshape(field.shape)


def solution(mesh):
    devices = mesh.devices
    space, mode = devices.shape
    fine = Mesh(devices.reshape(4, space // 4, mode // 2, 2), SPACE + MODE)
    in_specs = (P(MODE, SPACE, None), P(MODE, SPACE, None), P(None, MODE), P(MODE), P())
    out_specs = P(MODE, SPACE, None)
    return jax.shard_map(
        per_device, mesh=fine, in_specs=in_specs, out_specs=out_specs, check_vma=False
    )
```

```python
import functools

import jax
import jax.numpy as jnp
from jax import lax
from jax.experimental import pallas as pl
from jax.experimental.pallas import tpu as pltpu
from jax.sharding import Mesh
from jax.sharding import PartitionSpec as P

NXY = 16
SUBSTEPS = 3
HALO = SUBSTEPS

courant = 0.3
time_step = 0.5


SPACE = ("sx", "sy")
MODE = ("mz", "mc")


def neighbours(field):
    rows, planes, cells = field.shape
    grid = field.reshape(rows, planes, NXY, NXY)
    padded = jnp.pad(grid, ((0, 0), (0, 0), (1, 1), (1, 1)))
    lower_x = padded[:, :, :-2, 1:-1].reshape(field.shape)
    upper_x = padded[:, :, 2:, 1:-1].reshape(field.shape)
    lower_y = padded[:, :, 1:-1, :-2].reshape(field.shape)
    upper_y = padded[:, :, 1:-1, 2:].reshape(field.shape)
    return (lower_x, upper_x, lower_y, upper_y)


def upwind(field, below, above, velocity):
    lower_x, upper_x, lower_y, upper_y = neighbours(field)
    lowers = [lower_x, lower_y, below]
    uppers = [upper_x, upper_y, above]
    flux = jnp.zeros_like(field)
    for direction in range(3):
        speed = velocity[direction][:, None, None]
        flux = flux + jnp.maximum(speed, 0.0) * (field - lowers[direction])
        flux = flux + jnp.minimum(speed, 0.0) * (uppers[direction] - field)
    return field - courant * flux


def with_halo(block, sides, width):
    for axis, dim in sides:
        count = lax.axis_size(axis)
        forward = [(i, i + 1) for i in range(count - 1)]
        backward = [(target, source) for source, target in forward]
        low = lax.ppermute(
            lax.slice_in_dim(block, block.shape[dim] - width, None, axis=dim), axis, forward
        )
        high = lax.ppermute(lax.slice_in_dim(block, 0, width, axis=dim), axis, backward)
        block = jnp.concatenate([low, block, high], axis=dim)
    return block


def plane_step(f, lower_z, upper_z, vel, x_lo, x_hi, y_lo, y_hi):
    cells = f.shape[-1]
    zero = jnp.zeros_like(f)
    lower_x = jnp.where(x_lo, zero, pltpu.roll(f, NXY, 1))
    upper_x = jnp.where(x_hi, zero, pltpu.roll(f, cells - NXY, 1))
    lower_y = jnp.where(y_lo, zero, pltpu.roll(f, 1, 1))
    upper_y = jnp.where(y_hi, zero, pltpu.roll(f, cells - 1, 1))
    lowers = [lower_x, lower_y, lower_z]
    uppers = [upper_x, upper_y, upper_z]
    flux = jnp.zeros_like(f)
    for direction in range(3):
        speed = vel[direction]
        flux = flux + jnp.maximum(speed, 0.0) * (f - lowers[direction])
        flux = flux + jnp.minimum(speed, 0.0) * (uppers[direction] - f)
    return f - courant * flux


def transport_kernel(pos_ref, b2_ref, b1_ref, d_ref, a1_ref, a2_ref, v_ref, gl_ref, gh_ref, o_ref, *, total_planes):
    depth = d_ref.shape[1]
    halo = SUBSTEPS
    extra = halo - depth
    planes = [b2_ref[:, depth - extra + i, :] for i in range(extra)]
    planes += [b1_ref[:, p, :] for p in range(depth)]
    planes += [d_ref[:, p, :] for p in range(depth)]
    planes += [a1_ref[:, p, :] for p in range(depth)]
    planes += [a2_ref[:, i, :] for i in range(extra)]
    rows, cells = planes[0].shape
    pos = pos_ref[0]
    gl = gl_ref[...]
    gh = gh_ref[...]
    vel = [v_ref[d] for d in range(3)]
    lane = lax.broadcasted_iota(jnp.int32, (rows, cells), 1)
    y = lane % NXY
    x = lane // NXY
    x_lo, x_hi, y_lo, y_hi = x == 0, x == NXY - 1, y == 0, y == NXY - 1

    def fix(e, f):
        z = pos * depth - halo + e
        f = jnp.where(z < 0, gl, f)
        return jnp.where(z >= total_planes, gh, f)

    field = [fix(e, f) for e, f in enumerate(planes)]
    n = len(field)
    for t in range(1, SUBSTEPS + 1):
        new = [None] * n
        for e in range(t, n - t):
            new[e] = fix(e, plane_step(field[e], field[e - 1], field[e + 1], vel, x_lo, x_hi, y_lo, y_hi))
        field = new
    for p in range(depth):
        o_ref[:, p, :] = field[halo + p]


def run_transport(pos, b2, b1, d, a1, a2, vel3, gl, gh, total_planes):
    rows, depth, cells = d.shape
    vmem = pltpu.VMEM
    spec = pl.BlockSpec(memory_space=vmem)
    return pl.pallas_call(
        functools.partial(transport_kernel, total_planes=total_planes),
        out_shape=jax.ShapeDtypeStruct(d.shape, d.dtype),
        in_specs=[pl.BlockSpec(memory_space=pltpu.SMEM)] + [spec] * 8,
        out_specs=spec,
    )(pos, b2, b1, d, a1, a2, vel3, gl, gh)


def gain_kernel(*refs, group, rows, pieces):
    t_refs = refs[:pieces]
    x_ref, xi_ref, o_ref = refs[pieces:]
    x = x_ref[...]
    tile = x.shape[-1]
    n_groups = o_ref.shape[1] // group

    def body(g, carry):
        start = pl.multiple_of(g * group * rows, group * rows)
        acc = None
        for p in range(pieces):
            t = t_refs[p][pl.ds(start, group * rows), :]
            inner = jnp.dot(t, x, preferred_element_type=jnp.float32)
            inner = inner.reshape(group, rows, tile)
            term = jnp.sum(inner * xi_ref[p].astype(jnp.float32)[None], axis=1)
            acc = term if acc is None else acc + term
        o_ref[0, pl.ds(pl.multiple_of(g * group, group), group), :] = acc
        return carry

    lax.fori_loop(0, n_groups, body, 0)


def contract(tensors, columns, factor, k_count, tile, group=8):
    kr, width = tensors[0].shape
    pieces = len(tensors)
    rows = kr // k_count
    total = columns.shape[1]
    kernel = functools.partial(gain_kernel, group=group, rows=rows, pieces=pieces)
    return pl.pallas_call(
        kernel,
        out_shape=jax.ShapeDtypeStruct((total // tile, k_count, tile), jnp.float32),
        grid=(total // tile,),
        in_specs=[pl.BlockSpec((kr, width), lambda c: (0, 0)) for _ in range(pieces)]
        + [
            pl.BlockSpec((width, tile), lambda c: (0, c)),
            pl.BlockSpec((pieces, rows, tile), lambda c: (0, 0, c)),
        ],
        out_specs=pl.BlockSpec((1, k_count, tile), lambda c: (c, 0, 0)),
        compiler_params=pltpu.CompilerParams(vmem_limit_bytes=48 * 1024 * 1024),
        cost_estimate=pl.CostEstimate(
            flops=2 * pieces * kr * width * total + 2 * pieces * kr * total,
            bytes_accessed=pieces * kr * width * 2 + width * total * 2 + pieces * rows * total * 2 + k_count * total * 4,
            transcendentals=0,
        ),
    )(*tensors, columns, factor)


def ring_pieces(x, axis):
    count = lax.axis_size(axis)
    return [x] + [
        lax.ppermute(x, axis, [(i, (i + d) % count) for i in range(count)]) for d in range(1, count)
    ]


def ring_sum_back(partial, axis):
    count = lax.axis_size(axis)
    total = partial[0]
    for d in range(1, count):
        total = total + lax.ppermute(partial[d], axis, [(i, (i - d) % count) for i in range(count)])
    return total


def swap_pair(x):
    return lax.ppermute(x, "mc", [(0, 1), (1, 0)])


def in_core_order(first_core, mine, other, axis):
    a = jnp.concatenate([mine, other], axis=axis)
    b = jnp.concatenate([other, mine], axis=axis)
    return jnp.where(first_core, a, b)


def per_device(density, tensor, velocity, inflow, flags):
    rows, depth, cells = density.shape
    position = lax.axis_index(SPACE)
    final = lax.axis_size(SPACE) - 1
    ghost_low = flags[0].astype(jnp.float32)[None, :] * inflow[:, None]
    ghost_high = flags[1].astype(jnp.float32)[None, :] * inflow[:, None]

    count = lax.axis_size(SPACE)
    halo_from = lambda d: lax.ppermute(
        density, SPACE, [(i, i + d) for i in range(max(0, -d), min(count, count - d))]
    )
    halos = [halo_from(2), halo_from(1), halo_from(-1), halo_from(-2)]
    halos, tensor = lax.optimization_barrier((halos, tensor))
    k_count, i_count, width = tensor.shape
    tensors = ring_pieces(tensor.reshape(k_count * i_count, width), "sy")
    field = run_transport(
        position.reshape(1).astype(jnp.int32),
        halos[0],
        halos[1],
        density,
        halos[2],
        halos[3],
        velocity[:, :, None],
        ghost_low,
        ghost_high,
        count * depth,
    )

    coarse = field.astype(jnp.bfloat16)
    pair_modes = lax.all_gather(coarse, "mc", axis=0, tiled=True)
    all_modes = lax.all_gather(pair_modes, "mz", axis=0, tiled=True)
    modes = all_modes.shape[0]
    pieces = ring_pieces(all_modes.reshape(modes, -1), "sx")
    pieces, tensors = lax.optimization_barrier((pieces, tensors))
    columns = jnp.concatenate(pieces, axis=1)

    sx = lax.axis_index("sx")
    sy = lax.axis_index("sy")
    ny = lax.axis_size("sy")
    factor = jnp.stack(
        [
            lax.dynamic_slice_in_dim(
                columns, (sx * ny + (sy - d) % ny) * i_count, i_count, axis=0
            )
            for d in range(ny)
        ]
    )
    partial = contract(tensors, columns, factor, k_count, depth * cells)
    gain = ring_sum_back(partial, "sx")
    return field + time_step * gain.reshape(field.shape)


def solution(mesh):
    devices = mesh.devices
    space, mode = devices.shape
    fine = Mesh(devices.reshape(4, space // 4, mode // 2, 2), SPACE + MODE)
    in_specs = (P(MODE, SPACE, None), P(MODE, SPACE, None), P(None, MODE), P(MODE), P())
    out_specs = P(MODE, SPACE, None)
    return jax.shard_map(
        per_device, mesh=fine, in_specs=in_specs, out_specs=out_specs, check_vma=False
    )
```

```python
import functools

import jax
import jax.numpy as jnp
from jax import lax
from jax.experimental import pallas as pl
from jax.experimental.pallas import tpu as pltpu
from jax.sharding import Mesh
from jax.sharding import PartitionSpec as P

NXY = 16
SUBSTEPS = 3
HALO = SUBSTEPS

courant = 0.3
time_step = 0.5


SPACE = ("sx", "sy")
MODE = ("mz", "mc")


def neighbours(field):
    rows, planes, cells = field.shape
    grid = field.reshape(rows, planes, NXY, NXY)
    padded = jnp.pad(grid, ((0, 0), (0, 0), (1, 1), (1, 1)))
    lower_x = padded[:, :, :-2, 1:-1].reshape(field.shape)
    upper_x = padded[:, :, 2:, 1:-1].reshape(field.shape)
    lower_y = padded[:, :, 1:-1, :-2].reshape(field.shape)
    upper_y = padded[:, :, 1:-1, 2:].reshape(field.shape)
    return (lower_x, upper_x, lower_y, upper_y)


def upwind(field, below, above, velocity):
    lower_x, upper_x, lower_y, upper_y = neighbours(field)
    lowers = [lower_x, lower_y, below]
    uppers = [upper_x, upper_y, above]
    flux = jnp.zeros_like(field)
    for direction in range(3):
        speed = velocity[direction][:, None, None]
        flux = flux + jnp.maximum(speed, 0.0) * (field - lowers[direction])
        flux = flux + jnp.minimum(speed, 0.0) * (uppers[direction] - field)
    return field - courant * flux


def with_halo(block, sides, width):
    for axis, dim in sides:
        count = lax.axis_size(axis)
        forward = [(i, i + 1) for i in range(count - 1)]
        backward = [(target, source) for source, target in forward]
        low = lax.ppermute(
            lax.slice_in_dim(block, block.shape[dim] - width, None, axis=dim), axis, forward
        )
        high = lax.ppermute(lax.slice_in_dim(block, 0, width, axis=dim), axis, backward)
        block = jnp.concatenate([low, block, high], axis=dim)
    return block


def plane_step(f, lower_z, upper_z, vel, x_lo, x_hi, y_lo, y_hi):
    cells = f.shape[-1]
    zero = jnp.zeros_like(f)
    lower_x = jnp.where(x_lo, zero, pltpu.roll(f, NXY, 1))
    upper_x = jnp.where(x_hi, zero, pltpu.roll(f, cells - NXY, 1))
    lower_y = jnp.where(y_lo, zero, pltpu.roll(f, 1, 1))
    upper_y = jnp.where(y_hi, zero, pltpu.roll(f, cells - 1, 1))
    lowers = [lower_x, lower_y, lower_z]
    uppers = [upper_x, upper_y, upper_z]
    flux = jnp.zeros_like(f)
    for direction in range(3):
        speed = vel[direction]
        flux = flux + jnp.maximum(speed, 0.0) * (f - lowers[direction])
        flux = flux + jnp.minimum(speed, 0.0) * (uppers[direction] - f)
    return f - courant * flux


def transport_kernel(pos_ref, b2_ref, b1_ref, d_ref, a1_ref, a2_ref, v_ref, gl_ref, gh_ref, o_ref, *, total_planes):
    depth = d_ref.shape[1]
    halo = SUBSTEPS
    extra = halo - depth
    planes = [b2_ref[:, depth - extra + i, :] for i in range(extra)]
    planes += [b1_ref[:, p, :] for p in range(depth)]
    planes += [d_ref[:, p, :] for p in range(depth)]
    planes += [a1_ref[:, p, :] for p in range(depth)]
    planes += [a2_ref[:, i, :] for i in range(extra)]
    rows, cells = planes[0].shape
    pos = pos_ref[0]
    gl = gl_ref[...]
    gh = gh_ref[...]
    vel = [v_ref[d] for d in range(3)]
    lane = lax.broadcasted_iota(jnp.int32, (rows, cells), 1)
    y = lane % NXY
    x = lane // NXY
    x_lo, x_hi, y_lo, y_hi = x == 0, x == NXY - 1, y == 0, y == NXY - 1

    def fix(e, f):
        z = pos * depth - halo + e
        f = jnp.where(z < 0, gl, f)
        return jnp.where(z >= total_planes, gh, f)

    field = [fix(e, f) for e, f in enumerate(planes)]
    n = len(field)
    for t in range(1, SUBSTEPS + 1):
        new = [None] * n
        for e in range(t, n - t):
            new[e] = fix(e, plane_step(field[e], field[e - 1], field[e + 1], vel, x_lo, x_hi, y_lo, y_hi))
        field = new
    for p in range(depth):
        o_ref[:, p, :] = field[halo + p]


def run_transport(pos, b2, b1, d, a1, a2, vel3, gl, gh, total_planes):
    rows, depth, cells = d.shape
    vmem = pltpu.VMEM
    spec = pl.BlockSpec(memory_space=vmem)
    return pl.pallas_call(
        functools.partial(transport_kernel, total_planes=total_planes),
        out_shape=jax.ShapeDtypeStruct(d.shape, d.dtype),
        in_specs=[pl.BlockSpec(memory_space=pltpu.SMEM)] + [spec] * 8,
        out_specs=spec,
    )(pos, b2, b1, d, a1, a2, vel3, gl, gh)


def gain_kernel(row_ref, *refs, group, rows, pieces):
    t_refs = refs[:pieces]
    x_refs = refs[pieces : 2 * pieces]
    o_ref = refs[2 * pieces]
    n_groups = o_ref.shape[1] // group
    column = pl.program_id(0)

    def run(x_ref):
        x = x_ref[...]
        tile = x.shape[-1]
        xis = [
            x_ref[pl.ds(pl.multiple_of(row_ref[d], rows), rows), :].astype(jnp.float32)
            for d in range(pieces)
        ]

        def body(g, carry):
            start = pl.multiple_of(g * group * rows, group * rows)
            acc = None
            for d in range(pieces):
                t = t_refs[d][pl.ds(start, group * rows), :]
                inner = jnp.dot(t, x, preferred_element_type=jnp.float32)
                inner = inner.reshape(group, rows, tile)
                term = jnp.sum(inner * xis[d][None], axis=1)
                acc = term if acc is None else acc + term
            o_ref[0, pl.ds(pl.multiple_of(g * group, group), group), :] = acc
            return carry

        lax.fori_loop(0, n_groups, body, 0)

    for p in range(len(x_refs)):
        pl.when(column == p)(functools.partial(run, x_refs[p]))


def contract(row_starts, tensors, columns, k_count, group=8):
    kr, width = tensors[0].shape
    pieces = len(tensors)
    rows = kr // k_count
    tile = columns[0].shape[1]
    total = tile * len(columns)
    kernel = functools.partial(gain_kernel, group=group, rows=rows, pieces=pieces)
    return pl.pallas_call(
        kernel,
        out_shape=jax.ShapeDtypeStruct((len(columns), k_count, tile), jnp.float32),
        grid=(len(columns),),
        in_specs=[pl.BlockSpec(memory_space=pltpu.SMEM)]
        + [pl.BlockSpec((kr, width), lambda c: (0, 0)) for _ in range(pieces)]
        + [pl.BlockSpec((width, tile), lambda c: (0, 0)) for _ in columns],
        out_specs=pl.BlockSpec((1, k_count, tile), lambda c: (c, 0, 0)),
        compiler_params=pltpu.CompilerParams(vmem_limit_bytes=48 * 1024 * 1024),
        cost_estimate=pl.CostEstimate(
            flops=2 * pieces * kr * width * total + 2 * pieces * kr * total,
            bytes_accessed=pieces * kr * width * 2 + width * total * 2 + k_count * total * 4,
            transcendentals=0,
        ),
    )(row_starts, *tensors, *columns)


def ring_pieces(x, axis):
    count = lax.axis_size(axis)
    return [x] + [
        lax.ppermute(x, axis, [(i, (i + d) % count) for i in range(count)]) for d in range(1, count)
    ]


def ring_sum_back(partial, axis):
    count = lax.axis_size(axis)
    total = partial[0]
    for d in range(1, count):
        total = total + lax.ppermute(partial[d], axis, [(i, (i - d) % count) for i in range(count)])
    return total


def swap_pair(x):
    return lax.ppermute(x, "mc", [(0, 1), (1, 0)])


def in_core_order(first_core, mine, other, axis):
    a = jnp.concatenate([mine, other], axis=axis)
    b = jnp.concatenate([other, mine], axis=axis)
    return jnp.where(first_core, a, b)


def per_device(density, tensor, velocity, inflow, flags):
    rows, depth, cells = density.shape
    position = lax.axis_index(SPACE)
    final = lax.axis_size(SPACE) - 1
    ghost_low = flags[0].astype(jnp.float32)[None, :] * inflow[:, None]
    ghost_high = flags[1].astype(jnp.float32)[None, :] * inflow[:, None]

    count = lax.axis_size(SPACE)
    halo_from = lambda d: lax.ppermute(
        density, SPACE, [(i, i + d) for i in range(max(0, -d), min(count, count - d))]
    )
    halos = [halo_from(2), halo_from(1), halo_from(-1), halo_from(-2)]
    halos, tensor = lax.optimization_barrier((halos, tensor))
    k_count, i_count, width = tensor.shape
    tensors = ring_pieces(tensor.reshape(k_count * i_count, width), "sy")
    field = run_transport(
        position.reshape(1).astype(jnp.int32),
        halos[0],
        halos[1],
        density,
        halos[2],
        halos[3],
        velocity[:, :, None],
        ghost_low,
        ghost_high,
        count * depth,
    )

    coarse = field.astype(jnp.bfloat16)
    all_modes = lax.all_gather(coarse, MODE, axis=0, tiled=True)
    modes = all_modes.shape[0]
    pieces = ring_pieces(all_modes.reshape(modes, -1), "sx")
    pieces, tensors = lax.optimization_barrier((pieces, tensors))

    sx = lax.axis_index("sx")
    sy = lax.axis_index("sy")
    ny = lax.axis_size("sy")
    row_starts = jnp.stack([(sx * ny + (sy - d) % ny) * i_count for d in range(ny)]).astype(jnp.int32)
    partial = contract(row_starts, tensors, pieces, k_count)
    gain = ring_sum_back(partial, "sx")
    return field + time_step * gain.reshape(field.shape)


def solution(mesh):
    devices = mesh.devices
    space, mode = devices.shape
    fine = Mesh(devices.reshape(4, space // 4, mode // 2, 2), SPACE + MODE)
    in_specs = (P(MODE, SPACE, None), P(MODE, SPACE, None), P(None, MODE), P(MODE), P())
    out_specs = P(MODE, SPACE, None)
    return jax.shard_map(
        per_device, mesh=fine, in_specs=in_specs, out_specs=out_specs, check_vma=False
    )
```

```python
import functools

import jax
import jax.numpy as jnp
from jax import lax
from jax.experimental import pallas as pl
from jax.experimental.pallas import tpu as pltpu
from jax.sharding import Mesh
from jax.sharding import PartitionSpec as P

NXY = 16
SUBSTEPS = 3
HALO = SUBSTEPS

courant = 0.3
time_step = 0.5


SPACE = ("sx", "sy")
MODE = ("mz", "mc")


def neighbours(field):
    rows, planes, cells = field.shape
    grid = field.reshape(rows, planes, NXY, NXY)
    padded = jnp.pad(grid, ((0, 0), (0, 0), (1, 1), (1, 1)))
    lower_x = padded[:, :, :-2, 1:-1].reshape(field.shape)
    upper_x = padded[:, :, 2:, 1:-1].reshape(field.shape)
    lower_y = padded[:, :, 1:-1, :-2].reshape(field.shape)
    upper_y = padded[:, :, 1:-1, 2:].reshape(field.shape)
    return (lower_x, upper_x, lower_y, upper_y)


def upwind(field, below, above, velocity):
    lower_x, upper_x, lower_y, upper_y = neighbours(field)
    lowers = [lower_x, lower_y, below]
    uppers = [upper_x, upper_y, above]
    flux = jnp.zeros_like(field)
    for direction in range(3):
        speed = velocity[direction][:, None, None]
        flux = flux + jnp.maximum(speed, 0.0) * (field - lowers[direction])
        flux = flux + jnp.minimum(speed, 0.0) * (uppers[direction] - field)
    return field - courant * flux


def with_halo(block, sides, width):
    for axis, dim in sides:
        count = lax.axis_size(axis)
        forward = [(i, i + 1) for i in range(count - 1)]
        backward = [(target, source) for source, target in forward]
        low = lax.ppermute(
            lax.slice_in_dim(block, block.shape[dim] - width, None, axis=dim), axis, forward
        )
        high = lax.ppermute(lax.slice_in_dim(block, 0, width, axis=dim), axis, backward)
        block = jnp.concatenate([low, block, high], axis=dim)
    return block


def plane_step(f, lower_z, upper_z, vel, x_lo, x_hi, y_lo, y_hi):
    cells = f.shape[-1]
    zero = jnp.zeros_like(f)
    lower_x = jnp.where(x_lo, zero, pltpu.roll(f, NXY, 1))
    upper_x = jnp.where(x_hi, zero, pltpu.roll(f, cells - NXY, 1))
    lower_y = jnp.where(y_lo, zero, pltpu.roll(f, 1, 1))
    upper_y = jnp.where(y_hi, zero, pltpu.roll(f, cells - 1, 1))
    lowers = [lower_x, lower_y, lower_z]
    uppers = [upper_x, upper_y, upper_z]
    flux = jnp.zeros_like(f)
    for direction in range(3):
        speed = vel[direction]
        flux = flux + jnp.maximum(speed, 0.0) * (f - lowers[direction])
        flux = flux + jnp.minimum(speed, 0.0) * (uppers[direction] - f)
    return f - courant * flux


def transport_kernel(pos_ref, b2_ref, b1_ref, d_ref, a1_ref, a2_ref, v_ref, gl_ref, gh_ref, o_ref, *, total_planes):
    depth = d_ref.shape[1]
    halo = SUBSTEPS
    extra = halo - depth
    planes = [b2_ref[:, depth - extra + i, :] for i in range(extra)]
    planes += [b1_ref[:, p, :] for p in range(depth)]
    planes += [d_ref[:, p, :] for p in range(depth)]
    planes += [a1_ref[:, p, :] for p in range(depth)]
    planes += [a2_ref[:, i, :] for i in range(extra)]
    rows, cells = planes[0].shape
    pos = pos_ref[0]
    gl = gl_ref[...]
    gh = gh_ref[...]
    vel = [v_ref[d] for d in range(3)]
    lane = lax.broadcasted_iota(jnp.int32, (rows, cells), 1)
    y = lane % NXY
    x = lane // NXY
    x_lo, x_hi, y_lo, y_hi = x == 0, x == NXY - 1, y == 0, y == NXY - 1

    def fix(e, f):
        z = pos * depth - halo + e
        f = jnp.where(z < 0, gl, f)
        return jnp.where(z >= total_planes, gh, f)

    field = [fix(e, f) for e, f in enumerate(planes)]
    n = len(field)
    for t in range(1, SUBSTEPS + 1):
        new = [None] * n
        for e in range(t, n - t):
            new[e] = fix(e, plane_step(field[e], field[e - 1], field[e + 1], vel, x_lo, x_hi, y_lo, y_hi))
        field = new
    for p in range(depth):
        o_ref[:, p, :] = field[halo + p]


def run_transport(pos, b2, b1, d, a1, a2, vel3, gl, gh, total_planes):
    rows, depth, cells = d.shape
    vmem = pltpu.VMEM
    spec = pl.BlockSpec(memory_space=vmem)
    return pl.pallas_call(
        functools.partial(transport_kernel, total_planes=total_planes),
        out_shape=jax.ShapeDtypeStruct(d.shape, d.dtype),
        in_specs=[pl.BlockSpec(memory_space=pltpu.SMEM)] + [spec] * 8,
        out_specs=spec,
    )(pos, b2, b1, d, a1, a2, vel3, gl, gh)


def gain_kernel(row_ref, *refs, group, rows, pieces, halves):
    t_refs = refs[:pieces]
    n_x = len(refs) - pieces - 1
    x_refs = refs[pieces : pieces + n_x]
    o_ref = refs[pieces + n_x]
    n_groups = o_ref.shape[1] // group
    column = pl.program_id(0)
    half = pl.program_id(1)

    def run(x_ref):
        x = x_ref[...]
        tile = x.shape[-1]
        xis = [
            x_ref[pl.ds(pl.multiple_of(row_ref[d], rows), rows), :].astype(jnp.float32)
            for d in range(pieces)
        ]

        def body(g, carry):
            start = pl.multiple_of(g * group * rows, group * rows)
            acc = None
            for d in range(pieces):
                t = t_refs[d][pl.ds(start, group * rows), :]
                inner = jnp.dot(t, x, preferred_element_type=jnp.float32)
                inner = inner.reshape(group, rows, tile)
                term = jnp.sum(inner * xis[d][None], axis=1)
                acc = term if acc is None else acc + term
            o_ref[0, pl.ds(pl.multiple_of(g * group, group), group), :] = acc
            return carry

        lax.fori_loop(0, n_groups, body, 0)

    for p in range(n_x // halves):
        for h in range(halves):
            pl.when((column == p) & (half == h))(functools.partial(run, x_refs[p * halves + h]))


def contract(row_starts, tensors, columns, k_count, halves, group=8):
    kr, width = tensors[0].shape
    pieces = len(tensors)
    rows = kr // k_count
    tile = columns[0].shape[1]
    n_pieces = len(columns) // halves
    total = tile * len(columns)
    kernel = functools.partial(gain_kernel, group=group, rows=rows, pieces=pieces, halves=halves)
    return pl.pallas_call(
        kernel,
        out_shape=jax.ShapeDtypeStruct((n_pieces, k_count, halves * tile), jnp.float32),
        grid=(n_pieces, halves),
        in_specs=[pl.BlockSpec(memory_space=pltpu.SMEM)]
        + [pl.BlockSpec((kr, width), lambda c, h: (0, 0)) for _ in range(pieces)]
        + [pl.BlockSpec((width, tile), lambda c, h: (0, 0)) for _ in columns],
        out_specs=pl.BlockSpec((1, k_count, tile), lambda c, h: (c, 0, h)),
        compiler_params=pltpu.CompilerParams(vmem_limit_bytes=48 * 1024 * 1024),
        cost_estimate=pl.CostEstimate(
            flops=2 * pieces * kr * width * total + 2 * pieces * kr * total,
            bytes_accessed=pieces * kr * width * 2 + width * total * 2 + k_count * total * 4,
            transcendentals=0,
        ),
    )(row_starts, *tensors, *columns)


def ring_pieces(x, axis):
    count = lax.axis_size(axis)
    return [x] + [
        lax.ppermute(x, axis, [(i, (i + d) % count) for i in range(count)]) for d in range(1, count)
    ]


def ring_sum_back(partial, axis):
    count = lax.axis_size(axis)
    total = partial[0]
    for d in range(1, count):
        total = total + lax.ppermute(partial[d], axis, [(i, (i - d) % count) for i in range(count)])
    return total


def swap_pair(x):
    return lax.ppermute(x, "mc", [(0, 1), (1, 0)])


def in_core_order(first_core, mine, other, axis):
    a = jnp.concatenate([mine, other], axis=axis)
    b = jnp.concatenate([other, mine], axis=axis)
    return jnp.where(first_core, a, b)


def per_device(density, tensor, velocity, inflow, flags):
    rows, depth, cells = density.shape
    position = lax.axis_index(SPACE)
    final = lax.axis_size(SPACE) - 1
    ghost_low = flags[0].astype(jnp.float32)[None, :] * inflow[:, None]
    ghost_high = flags[1].astype(jnp.float32)[None, :] * inflow[:, None]

    count = lax.axis_size(SPACE)
    halo_from = lambda d: lax.ppermute(
        density, SPACE, [(i, i + d) for i in range(max(0, -d), min(count, count - d))]
    )
    halos = [halo_from(2), halo_from(1), halo_from(-1), halo_from(-2)]
    halos, tensor = lax.optimization_barrier((halos, tensor))
    k_count, i_count, width = tensor.shape
    tensors = ring_pieces(tensor.reshape(k_count * i_count, width), "sy")
    field = run_transport(
        position.reshape(1).astype(jnp.int32),
        halos[0],
        halos[1],
        density,
        halos[2],
        halos[3],
        velocity[:, :, None],
        ghost_low,
        ghost_high,
        count * depth,
    )

    coarse = field.astype(jnp.bfloat16)
    all_modes = lax.all_gather(coarse, MODE, axis=0, tiled=True)
    first_core = lax.axis_index("mc") == 0
    mine = jnp.where(first_core, all_modes[:, 0], all_modes[:, 1])
    fetched = ring_pieces(mine, "sx")[1:]
    fetched, tensors = lax.optimization_barrier((fetched, tensors))
    other = swap_pair(jnp.stack(fetched))
    columns = [all_modes[:, 0], all_modes[:, 1]]
    for d in range(len(fetched)):
        columns.append(jnp.where(first_core, fetched[d], other[d]))
        columns.append(jnp.where(first_core, other[d], fetched[d]))

    sx = lax.axis_index("sx")
    sy = lax.axis_index("sy")
    ny = lax.axis_size("sy")
    row_starts = jnp.stack([(sx * ny + (sy - d) % ny) * i_count for d in range(ny)]).astype(jnp.int32)
    partial = contract(row_starts, tensors, columns, k_count, depth)
    gain = ring_sum_back(partial, "sx")
    return field + time_step * gain.reshape(field.shape)


def solution(mesh):
    devices = mesh.devices
    space, mode = devices.shape
    fine = Mesh(devices.reshape(4, space // 4, mode // 2, 2), SPACE + MODE)
    in_specs = (P(MODE, SPACE, None), P(MODE, SPACE, None), P(None, MODE), P(MODE), P())
    out_specs = P(MODE, SPACE, None)
    return jax.shard_map(
        per_device, mesh=fine, in_specs=in_specs, out_specs=out_specs, check_vma=False
    )
```

```python
import functools

import jax
import jax.numpy as jnp
from jax import lax
from jax.experimental import pallas as pl
from jax.experimental.pallas import tpu as pltpu
from jax.sharding import Mesh
from jax.sharding import PartitionSpec as P

NXY = 16
SUBSTEPS = 3
HALO = SUBSTEPS

courant = 0.3
time_step = 0.5


SPACE = ("sx", "sy")
MODE = ("mz", "mc")


def neighbours(field):
    rows, planes, cells = field.shape
    grid = field.reshape(rows, planes, NXY, NXY)
    padded = jnp.pad(grid, ((0, 0), (0, 0), (1, 1), (1, 1)))
    lower_x = padded[:, :, :-2, 1:-1].reshape(field.shape)
    upper_x = padded[:, :, 2:, 1:-1].reshape(field.shape)
    lower_y = padded[:, :, 1:-1, :-2].reshape(field.shape)
    upper_y = padded[:, :, 1:-1, 2:].reshape(field.shape)
    return (lower_x, upper_x, lower_y, upper_y)


def upwind(field, below, above, velocity):
    lower_x, upper_x, lower_y, upper_y = neighbours(field)
    lowers = [lower_x, lower_y, below]
    uppers = [upper_x, upper_y, above]
    flux = jnp.zeros_like(field)
    for direction in range(3):
        speed = velocity[direction][:, None, None]
        flux = flux + jnp.maximum(speed, 0.0) * (field - lowers[direction])
        flux = flux + jnp.minimum(speed, 0.0) * (uppers[direction] - field)
    return field - courant * flux


def with_halo(block, sides, width):
    for axis, dim in sides:
        count = lax.axis_size(axis)
        forward = [(i, i + 1) for i in range(count - 1)]
        backward = [(target, source) for source, target in forward]
        low = lax.ppermute(
            lax.slice_in_dim(block, block.shape[dim] - width, None, axis=dim), axis, forward
        )
        high = lax.ppermute(lax.slice_in_dim(block, 0, width, axis=dim), axis, backward)
        block = jnp.concatenate([low, block, high], axis=dim)
    return block


def plane_step(f, lower_z, upper_z, vel, x_lo, x_hi, y_lo, y_hi):
    cells = f.shape[-1]
    zero = jnp.zeros_like(f)
    lower_x = jnp.where(x_lo, zero, pltpu.roll(f, NXY, 1))
    upper_x = jnp.where(x_hi, zero, pltpu.roll(f, cells - NXY, 1))
    lower_y = jnp.where(y_lo, zero, pltpu.roll(f, 1, 1))
    upper_y = jnp.where(y_hi, zero, pltpu.roll(f, cells - 1, 1))
    lowers = [lower_x, lower_y, lower_z]
    uppers = [upper_x, upper_y, upper_z]
    flux = jnp.zeros_like(f)
    for direction in range(3):
        speed = vel[direction]
        flux = flux + jnp.maximum(speed, 0.0) * (f - lowers[direction])
        flux = flux + jnp.minimum(speed, 0.0) * (uppers[direction] - f)
    return f - courant * flux


def transport_kernel(pos_ref, b2_ref, b1_ref, d_ref, a1_ref, a2_ref, v_ref, gl_ref, gh_ref, o_ref, *, total_planes):
    depth = d_ref.shape[1]
    halo = SUBSTEPS
    extra = halo - depth
    planes = [b2_ref[:, depth - extra + i, :] for i in range(extra)]
    planes += [b1_ref[:, p, :] for p in range(depth)]
    planes += [d_ref[:, p, :] for p in range(depth)]
    planes += [a1_ref[:, p, :] for p in range(depth)]
    planes += [a2_ref[:, i, :] for i in range(extra)]
    rows, cells = planes[0].shape
    pos = pos_ref[0]
    gl = gl_ref[...]
    gh = gh_ref[...]
    vel = [v_ref[d] for d in range(3)]
    lane = lax.broadcasted_iota(jnp.int32, (rows, cells), 1)
    y = lane % NXY
    x = lane // NXY
    x_lo, x_hi, y_lo, y_hi = x == 0, x == NXY - 1, y == 0, y == NXY - 1

    def fix(e, f):
        z = pos * depth - halo + e
        f = jnp.where(z < 0, gl, f)
        return jnp.where(z >= total_planes, gh, f)

    field = [fix(e, f) for e, f in enumerate(planes)]
    n = len(field)
    for t in range(1, SUBSTEPS + 1):
        new = [None] * n
        for e in range(t, n - t):
            new[e] = fix(e, plane_step(field[e], field[e - 1], field[e + 1], vel, x_lo, x_hi, y_lo, y_hi))
        field = new
    for p in range(depth):
        o_ref[:, p, :] = field[halo + p]


def run_transport(pos, b2, b1, d, a1, a2, vel3, gl, gh, total_planes):
    rows, depth, cells = d.shape
    vmem = pltpu.VMEM
    spec = pl.BlockSpec(memory_space=vmem)
    return pl.pallas_call(
        functools.partial(transport_kernel, total_planes=total_planes),
        out_shape=jax.ShapeDtypeStruct(d.shape, d.dtype),
        in_specs=[pl.BlockSpec(memory_space=pltpu.SMEM)] + [spec] * 8,
        out_specs=spec,
    )(pos, b2, b1, d, a1, a2, vel3, gl, gh)


def gain_kernel(row_ref, *refs, group, rows, pieces, halves):
    t_refs = refs[:pieces]
    n_x = len(refs) - pieces - 1
    x_refs = refs[pieces : pieces + n_x]
    o_ref = refs[pieces + n_x]
    n_groups = o_ref.shape[1] // group
    column = pl.program_id(0)

    def run(x_group):
        x = jnp.concatenate([r[...] for r in x_group], axis=1)
        tile = x.shape[-1]
        xis = [
            jnp.concatenate(
                [r[pl.ds(pl.multiple_of(row_ref[d], rows), rows), :] for r in x_group], axis=1
            ).astype(jnp.float32)
            for d in range(pieces)
        ]

        def body(g, carry):
            start = pl.multiple_of(g * group * rows, group * rows)
            acc = None
            for d in range(pieces):
                t = t_refs[d][pl.ds(start, group * rows), :]
                inner = jnp.dot(t, x, preferred_element_type=jnp.float32)
                inner = inner.reshape(group, rows, tile)
                term = jnp.sum(inner * xis[d][None], axis=1)
                acc = term if acc is None else acc + term
            o_ref[0, pl.ds(pl.multiple_of(g * group, group), group), :] = acc
            return carry

        lax.fori_loop(0, n_groups, body, 0)

    for p in range(n_x // halves):
        group_refs = x_refs[p * halves : (p + 1) * halves]
        pl.when(column == p)(functools.partial(run, group_refs))


def contract(row_starts, tensors, columns, k_count, halves, group=8):
    kr, width = tensors[0].shape
    pieces = len(tensors)
    rows = kr // k_count
    tile = columns[0].shape[1]
    n_pieces = len(columns) // halves
    total = tile * len(columns)
    kernel = functools.partial(gain_kernel, group=group, rows=rows, pieces=pieces, halves=halves)
    return pl.pallas_call(
        kernel,
        out_shape=jax.ShapeDtypeStruct((n_pieces, k_count, halves * tile), jnp.float32),
        grid=(n_pieces,),
        in_specs=[pl.BlockSpec(memory_space=pltpu.SMEM)]
        + [pl.BlockSpec((kr, width), lambda c: (0, 0)) for _ in range(pieces)]
        + [pl.BlockSpec((width, tile), lambda c: (0, 0)) for _ in columns],
        out_specs=pl.BlockSpec((1, k_count, halves * tile), lambda c: (c, 0, 0)),
        compiler_params=pltpu.CompilerParams(vmem_limit_bytes=48 * 1024 * 1024),
        cost_estimate=pl.CostEstimate(
            flops=2 * pieces * kr * width * total + 2 * pieces * kr * total,
            bytes_accessed=pieces * kr * width * 2 + width * total * 2 + k_count * total * 4,
            transcendentals=0,
        ),
    )(row_starts, *tensors, *columns)


def ring_pieces(x, axis):
    count = lax.axis_size(axis)
    return [x] + [
        lax.ppermute(x, axis, [(i, (i + d) % count) for i in range(count)]) for d in range(1, count)
    ]


def ring_sum_back(partial, axis):
    count = lax.axis_size(axis)
    total = partial[0]
    for d in range(1, count):
        total = total + lax.ppermute(partial[d], axis, [(i, (i - d) % count) for i in range(count)])
    return total


def swap_pair(x):
    return lax.ppermute(x, "mc", [(0, 1), (1, 0)])


def in_core_order(first_core, mine, other, axis):
    a = jnp.concatenate([mine, other], axis=axis)
    b = jnp.concatenate([other, mine], axis=axis)
    return jnp.where(first_core, a, b)


def per_device(density, tensor, velocity, inflow, flags):
    rows, depth, cells = density.shape
    position = lax.axis_index(SPACE)
    final = lax.axis_size(SPACE) - 1
    ghost_low = flags[0].astype(jnp.float32)[None, :] * inflow[:, None]
    ghost_high = flags[1].astype(jnp.float32)[None, :] * inflow[:, None]

    count = lax.axis_size(SPACE)
    halo_from = lambda d: lax.ppermute(
        density, SPACE, [(i, i + d) for i in range(max(0, -d), min(count, count - d))]
    )
    halos = [halo_from(2), halo_from(1), halo_from(-1), halo_from(-2)]
    halos, tensor = lax.optimization_barrier((halos, tensor))
    k_count, i_count, width = tensor.shape
    tensors = ring_pieces(tensor.reshape(k_count * i_count, width), "sy")
    field = run_transport(
        position.reshape(1).astype(jnp.int32),
        halos[0],
        halos[1],
        density,
        halos[2],
        halos[3],
        velocity[:, :, None],
        ghost_low,
        ghost_high,
        count * depth,
    )

    coarse = field.astype(jnp.bfloat16)
    all_modes = lax.all_gather(coarse, MODE, axis=0, tiled=True)
    first_core = lax.axis_index("mc") == 0
    mine = jnp.where(first_core, all_modes[:, 0], all_modes[:, 1])
    fetched = ring_pieces(mine, "sx")[1:]
    fetched, tensors = lax.optimization_barrier((fetched, tensors))
    other = swap_pair(jnp.stack(fetched))
    columns = [all_modes[:, 0], all_modes[:, 1]]
    for d in range(len(fetched)):
        columns.append(jnp.where(first_core, fetched[d], other[d]))
        columns.append(jnp.where(first_core, other[d], fetched[d]))

    sx = lax.axis_index("sx")
    sy = lax.axis_index("sy")
    ny = lax.axis_size("sy")
    row_starts = jnp.stack([(sx * ny + (sy - d) % ny) * i_count for d in range(ny)]).astype(jnp.int32)
    partial = contract(row_starts, tensors, columns, k_count, depth)
    gain = ring_sum_back(partial, "sx")
    return field + time_step * gain.reshape(field.shape)


def solution(mesh):
    devices = mesh.devices
    space, mode = devices.shape
    fine = Mesh(devices.reshape(4, space // 4, mode // 2, 2), SPACE + MODE)
    in_specs = (P(MODE, SPACE, None), P(MODE, SPACE, None), P(None, MODE), P(MODE), P())
    out_specs = P(MODE, SPACE, None)
    return jax.shard_map(
        per_device, mesh=fine, in_specs=in_specs, out_specs=out_specs, check_vma=False
    )
```

```python
import functools

import jax
import jax.numpy as jnp
from jax import lax
from jax.experimental import pallas as pl
from jax.experimental.pallas import tpu as pltpu
from jax.sharding import Mesh
from jax.sharding import PartitionSpec as P

NXY = 16
SUBSTEPS = 3
HALO = SUBSTEPS

courant = 0.3
time_step = 0.5


SPACE = ("sx", "sy")
MODE = ("mz", "mc")


def neighbours(field):
    rows, planes, cells = field.shape
    grid = field.reshape(rows, planes, NXY, NXY)
    padded = jnp.pad(grid, ((0, 0), (0, 0), (1, 1), (1, 1)))
    lower_x = padded[:, :, :-2, 1:-1].reshape(field.shape)
    upper_x = padded[:, :, 2:, 1:-1].reshape(field.shape)
    lower_y = padded[:, :, 1:-1, :-2].reshape(field.shape)
    upper_y = padded[:, :, 1:-1, 2:].reshape(field.shape)
    return (lower_x, upper_x, lower_y, upper_y)


def upwind(field, below, above, velocity):
    lower_x, upper_x, lower_y, upper_y = neighbours(field)
    lowers = [lower_x, lower_y, below]
    uppers = [upper_x, upper_y, above]
    flux = jnp.zeros_like(field)
    for direction in range(3):
        speed = velocity[direction][:, None, None]
        flux = flux + jnp.maximum(speed, 0.0) * (field - lowers[direction])
        flux = flux + jnp.minimum(speed, 0.0) * (uppers[direction] - field)
    return field - courant * flux


def with_halo(block, sides, width):
    for axis, dim in sides:
        count = lax.axis_size(axis)
        forward = [(i, i + 1) for i in range(count - 1)]
        backward = [(target, source) for source, target in forward]
        low = lax.ppermute(
            lax.slice_in_dim(block, block.shape[dim] - width, None, axis=dim), axis, forward
        )
        high = lax.ppermute(lax.slice_in_dim(block, 0, width, axis=dim), axis, backward)
        block = jnp.concatenate([low, block, high], axis=dim)
    return block


def plane_step(f, lower_z, upper_z, vel, x_lo, x_hi, y_lo, y_hi):
    cells = f.shape[-1]
    zero = jnp.zeros_like(f)
    lower_x = jnp.where(x_lo, zero, pltpu.roll(f, NXY, 1))
    upper_x = jnp.where(x_hi, zero, pltpu.roll(f, cells - NXY, 1))
    lower_y = jnp.where(y_lo, zero, pltpu.roll(f, 1, 1))
    upper_y = jnp.where(y_hi, zero, pltpu.roll(f, cells - 1, 1))
    lowers = [lower_x, lower_y, lower_z]
    uppers = [upper_x, upper_y, upper_z]
    flux = jnp.zeros_like(f)
    for direction in range(3):
        speed = vel[direction]
        flux = flux + jnp.maximum(speed, 0.0) * (f - lowers[direction])
        flux = flux + jnp.minimum(speed, 0.0) * (uppers[direction] - f)
    return f - courant * flux


def transport_kernel(pos_ref, b2_ref, b1_ref, d_ref, a1_ref, a2_ref, v_ref, gl_ref, gh_ref, o_ref, *, total_planes):
    depth = d_ref.shape[1]
    halo = SUBSTEPS
    extra = halo - depth
    planes = [b2_ref[:, depth - extra + i, :] for i in range(extra)]
    planes += [b1_ref[:, p, :] for p in range(depth)]
    planes += [d_ref[:, p, :] for p in range(depth)]
    planes += [a1_ref[:, p, :] for p in range(depth)]
    planes += [a2_ref[:, i, :] for i in range(extra)]
    rows, cells = planes[0].shape
    pos = pos_ref[0]
    gl = gl_ref[...]
    gh = gh_ref[...]
    vel = [v_ref[d] for d in range(3)]
    lane = lax.broadcasted_iota(jnp.int32, (rows, cells), 1)
    y = lane % NXY
    x = lane // NXY
    x_lo, x_hi, y_lo, y_hi = x == 0, x == NXY - 1, y == 0, y == NXY - 1

    def fix(e, f):
        z = pos * depth - halo + e
        f = jnp.where(z < 0, gl, f)
        return jnp.where(z >= total_planes, gh, f)

    field = [fix(e, f) for e, f in enumerate(planes)]
    n = len(field)
    for t in range(1, SUBSTEPS + 1):
        new = [None] * n
        for e in range(t, n - t):
            new[e] = fix(e, plane_step(field[e], field[e - 1], field[e + 1], vel, x_lo, x_hi, y_lo, y_hi))
        field = new
    for p in range(depth):
        o_ref[:, p, :] = field[halo + p]


def run_transport(pos, b2, b1, d, a1, a2, vel3, gl, gh, total_planes):
    rows, depth, cells = d.shape
    vmem = pltpu.VMEM
    spec = pl.BlockSpec(memory_space=vmem)
    return pl.pallas_call(
        functools.partial(transport_kernel, total_planes=total_planes),
        out_shape=jax.ShapeDtypeStruct(d.shape, d.dtype),
        in_specs=[pl.BlockSpec(memory_space=pltpu.SMEM)] + [spec] * 8,
        out_specs=spec,
    )(pos, b2, b1, d, a1, a2, vel3, gl, gh)


def gain_kernel(row_ref, *refs, group, rows, pieces, halves):
    t_refs = refs[:pieces]
    n_x = len(refs) - pieces - 1
    x_refs = refs[pieces : pieces + n_x]
    o_ref = refs[pieces + n_x]
    n_groups = o_ref.shape[1] // group
    column = pl.program_id(0)

    def run(x_group):
        x = jnp.concatenate([r[...] for r in x_group], axis=1)
        tile = x.shape[-1]
        xis = [
            jnp.concatenate(
                [r[pl.ds(pl.multiple_of(row_ref[d], rows), rows), :] for r in x_group], axis=1
            ).astype(jnp.float32)
            for d in range(pieces)
        ]

        def body(g, carry):
            start = pl.multiple_of(g * group * rows, group * rows)
            acc = None
            for d in range(pieces):
                t = t_refs[d][pl.ds(start, group * rows), :]
                inner = jnp.dot(t, x, preferred_element_type=jnp.float32)
                inner = inner.reshape(group, rows, tile)
                term = jnp.sum(inner * xis[d][None], axis=1)
                acc = term if acc is None else acc + term
            o_ref[0, pl.ds(pl.multiple_of(g * group, group), group), :] = acc
            return carry

        lax.fori_loop(0, n_groups, body, 0)

    for p in range(n_x // halves):
        group_refs = x_refs[p * halves : (p + 1) * halves]
        pl.when(column == p)(functools.partial(run, group_refs))


def contract(row_starts, tensors, columns, k_count, halves, group=16):
    kr, width = tensors[0].shape
    pieces = len(tensors)
    rows = kr // k_count
    tile = columns[0].shape[1]
    n_pieces = len(columns) // halves
    total = tile * len(columns)
    kernel = functools.partial(gain_kernel, group=group, rows=rows, pieces=pieces, halves=halves)
    return pl.pallas_call(
        kernel,
        out_shape=jax.ShapeDtypeStruct((n_pieces, k_count, halves * tile), jnp.float32),
        grid=(n_pieces,),
        in_specs=[pl.BlockSpec(memory_space=pltpu.SMEM)]
        + [pl.BlockSpec((kr, width), lambda c: (0, 0)) for _ in range(pieces)]
        + [pl.BlockSpec((width, tile), lambda c: (0, 0)) for _ in columns],
        out_specs=pl.BlockSpec((1, k_count, halves * tile), lambda c: (c, 0, 0)),
        compiler_params=pltpu.CompilerParams(vmem_limit_bytes=48 * 1024 * 1024),
        cost_estimate=pl.CostEstimate(
            flops=2 * pieces * kr * width * total + 2 * pieces * kr * total,
            bytes_accessed=pieces * kr * width * 2 + width * total * 2 + k_count * total * 4,
            transcendentals=0,
        ),
    )(row_starts, *tensors, *columns)


def ring_pieces(x, axis):
    count = lax.axis_size(axis)
    return [x] + [
        lax.ppermute(x, axis, [(i, (i + d) % count) for i in range(count)]) for d in range(1, count)
    ]


def ring_sum_back(partial, axis):
    count = lax.axis_size(axis)
    total = partial[0]
    for d in range(1, count):
        total = total + lax.ppermute(partial[d], axis, [(i, (i - d) % count) for i in range(count)])
    return total


def swap_pair(x):
    return lax.ppermute(x, "mc", [(0, 1), (1, 0)])


def in_core_order(first_core, mine, other, axis):
    a = jnp.concatenate([mine, other], axis=axis)
    b = jnp.concatenate([other, mine], axis=axis)
    return jnp.where(first_core, a, b)


def per_device(density, tensor, velocity, inflow, flags):
    rows, depth, cells = density.shape
    position = lax.axis_index(SPACE)
    final = lax.axis_size(SPACE) - 1
    ghost_low = flags[0].astype(jnp.float32)[None, :] * inflow[:, None]
    ghost_high = flags[1].astype(jnp.float32)[None, :] * inflow[:, None]

    count = lax.axis_size(SPACE)
    halo_from = lambda d: lax.ppermute(
        density, SPACE, [(i, i + d) for i in range(max(0, -d), min(count, count - d))]
    )
    halos = [halo_from(2), halo_from(1), halo_from(-1), halo_from(-2)]
    halos, tensor = lax.optimization_barrier((halos, tensor))
    k_count, i_count, width = tensor.shape
    tensors = ring_pieces(tensor.reshape(k_count * i_count, width), "sy")
    field = run_transport(
        position.reshape(1).astype(jnp.int32),
        halos[0],
        halos[1],
        density,
        halos[2],
        halos[3],
        velocity[:, :, None],
        ghost_low,
        ghost_high,
        count * depth,
    )

    coarse = field.astype(jnp.bfloat16)
    all_modes = lax.all_gather(coarse, MODE, axis=0, tiled=True)
    first_core = lax.axis_index("mc") == 0
    mine = jnp.where(first_core, all_modes[:, 0], all_modes[:, 1])
    fetched = ring_pieces(mine, "sx")[1:]
    fetched, tensors = lax.optimization_barrier((fetched, tensors))
    other = swap_pair(jnp.stack(fetched))
    columns = [all_modes[:, 0], all_modes[:, 1]]
    for d in range(len(fetched)):
        columns.append(jnp.where(first_core, fetched[d], other[d]))
        columns.append(jnp.where(first_core, other[d], fetched[d]))

    sx = lax.axis_index("sx")
    sy = lax.axis_index("sy")
    ny = lax.axis_size("sy")
    row_starts = jnp.stack([(sx * ny + (sy - d) % ny) * i_count for d in range(ny)]).astype(jnp.int32)
    partial = contract(row_starts, tensors, columns, k_count, depth)
    gain = ring_sum_back(partial, "sx")
    return field + time_step * gain.reshape(field.shape)


def solution(mesh):
    devices = mesh.devices
    space, mode = devices.shape
    fine = Mesh(devices.reshape(4, space // 4, mode // 2, 2), SPACE + MODE)
    in_specs = (P(MODE, SPACE, None), P(MODE, SPACE, None), P(None, MODE), P(MODE), P())
    out_specs = P(MODE, SPACE, None)
    return jax.shard_map(
        per_device, mesh=fine, in_specs=in_specs, out_specs=out_specs, check_vma=False
    )
```

```python
import functools

import jax
import jax.numpy as jnp
from jax import lax
from jax.experimental import pallas as pl
from jax.experimental.pallas import tpu as pltpu
from jax.sharding import Mesh
from jax.sharding import PartitionSpec as P

NXY = 16
SUBSTEPS = 3
HALO = SUBSTEPS

courant = 0.3
time_step = 0.5


SPACE = ("sx", "sy")
MODE = ("mz", "mc")


def neighbours(field):
    rows, planes, cells = field.shape
    grid = field.reshape(rows, planes, NXY, NXY)
    padded = jnp.pad(grid, ((0, 0), (0, 0), (1, 1), (1, 1)))
    lower_x = padded[:, :, :-2, 1:-1].reshape(field.shape)
    upper_x = padded[:, :, 2:, 1:-1].reshape(field.shape)
    lower_y = padded[:, :, 1:-1, :-2].reshape(field.shape)
    upper_y = padded[:, :, 1:-1, 2:].reshape(field.shape)
    return (lower_x, upper_x, lower_y, upper_y)


def upwind(field, below, above, velocity):
    lower_x, upper_x, lower_y, upper_y = neighbours(field)
    lowers = [lower_x, lower_y, below]
    uppers = [upper_x, upper_y, above]
    flux = jnp.zeros_like(field)
    for direction in range(3):
        speed = velocity[direction][:, None, None]
        flux = flux + jnp.maximum(speed, 0.0) * (field - lowers[direction])
        flux = flux + jnp.minimum(speed, 0.0) * (uppers[direction] - field)
    return field - courant * flux


def with_halo(block, sides, width):
    for axis, dim in sides:
        count = lax.axis_size(axis)
        forward = [(i, i + 1) for i in range(count - 1)]
        backward = [(target, source) for source, target in forward]
        low = lax.ppermute(
            lax.slice_in_dim(block, block.shape[dim] - width, None, axis=dim), axis, forward
        )
        high = lax.ppermute(lax.slice_in_dim(block, 0, width, axis=dim), axis, backward)
        block = jnp.concatenate([low, block, high], axis=dim)
    return block


def plane_step(f, lower_z, upper_z, vel, x_lo, x_hi, y_lo, y_hi):
    cells = f.shape[-1]
    zero = jnp.zeros_like(f)
    lower_x = jnp.where(x_lo, zero, pltpu.roll(f, NXY, 1))
    upper_x = jnp.where(x_hi, zero, pltpu.roll(f, cells - NXY, 1))
    lower_y = jnp.where(y_lo, zero, pltpu.roll(f, 1, 1))
    upper_y = jnp.where(y_hi, zero, pltpu.roll(f, cells - 1, 1))
    lowers = [lower_x, lower_y, lower_z]
    uppers = [upper_x, upper_y, upper_z]
    flux = jnp.zeros_like(f)
    for direction in range(3):
        speed = vel[direction]
        flux = flux + jnp.maximum(speed, 0.0) * (f - lowers[direction])
        flux = flux + jnp.minimum(speed, 0.0) * (uppers[direction] - f)
    return f - courant * flux


def transport_kernel(pos_ref, b2_ref, b1_ref, d_ref, a1_ref, a2_ref, v_ref, gl_ref, gh_ref, o_ref, *, total_planes):
    depth = d_ref.shape[1]
    halo = SUBSTEPS
    extra = halo - depth
    planes = [b2_ref[:, depth - extra + i, :] for i in range(extra)]
    planes += [b1_ref[:, p, :] for p in range(depth)]
    planes += [d_ref[:, p, :] for p in range(depth)]
    planes += [a1_ref[:, p, :] for p in range(depth)]
    planes += [a2_ref[:, i, :] for i in range(extra)]
    rows, cells = planes[0].shape
    pos = pos_ref[0]
    gl = gl_ref[...]
    gh = gh_ref[...]
    vel = [v_ref[d] for d in range(3)]
    lane = lax.broadcasted_iota(jnp.int32, (rows, cells), 1)
    y = lane % NXY
    x = lane // NXY
    x_lo, x_hi, y_lo, y_hi = x == 0, x == NXY - 1, y == 0, y == NXY - 1

    def fix(e, f):
        z = pos * depth - halo + e
        f = jnp.where(z < 0, gl, f)
        return jnp.where(z >= total_planes, gh, f)

    field = [fix(e, f) for e, f in enumerate(planes)]
    n = len(field)
    for t in range(1, SUBSTEPS + 1):
        new = [None] * n
        for e in range(t, n - t):
            new[e] = fix(e, plane_step(field[e], field[e - 1], field[e + 1], vel, x_lo, x_hi, y_lo, y_hi))
        field = new
    for p in range(depth):
        o_ref[:, p, :] = field[halo + p]


def run_transport(pos, b2, b1, d, a1, a2, vel3, gl, gh, total_planes):
    rows, depth, cells = d.shape
    vmem = pltpu.VMEM
    spec = pl.BlockSpec(memory_space=vmem)
    return pl.pallas_call(
        functools.partial(transport_kernel, total_planes=total_planes),
        out_shape=jax.ShapeDtypeStruct(d.shape, d.dtype),
        in_specs=[pl.BlockSpec(memory_space=pltpu.SMEM)] + [spec] * 8,
        out_specs=spec,
    )(pos, b2, b1, d, a1, a2, vel3, gl, gh)


def gain_kernel(row_ref, *refs, group, rows, pieces, halves):
    t_refs = refs[:pieces]
    n_x = len(refs) - pieces - 1
    x_refs = refs[pieces : pieces + n_x]
    o_ref = refs[pieces + n_x]
    n_groups = o_ref.shape[1] // group
    column = pl.program_id(0)

    def run(x_group):
        x = jnp.concatenate([r[...] for r in x_group], axis=1)
        tile = x.shape[-1]
        xis = [
            jnp.concatenate(
                [r[pl.ds(pl.multiple_of(row_ref[d], rows), rows), :] for r in x_group], axis=1
            ).astype(jnp.float32)
            for d in range(pieces)
        ]

        def body(g, carry):
            start = pl.multiple_of(g * group * rows, group * rows)
            acc = None
            for d in range(pieces):
                t = t_refs[d][pl.ds(start, group * rows), :]
                inner = jnp.dot(t, x, preferred_element_type=jnp.float32)
                inner = inner.reshape(group, rows, tile)
                term = jnp.sum(inner * xis[d][None], axis=1)
                acc = term if acc is None else acc + term
            o_ref[0, pl.ds(pl.multiple_of(g * group, group), group), :] = acc
            return carry

        lax.fori_loop(0, n_groups, body, 0)

    for p in range(n_x // halves):
        group_refs = x_refs[p * halves : (p + 1) * halves]
        pl.when(column == p)(functools.partial(run, group_refs))


def contract(row_starts, tensors, columns, k_count, halves, group=32):
    kr, width = tensors[0].shape
    pieces = len(tensors)
    rows = kr // k_count
    tile = columns[0].shape[1]
    n_pieces = len(columns) // halves
    total = tile * len(columns)
    kernel = functools.partial(gain_kernel, group=group, rows=rows, pieces=pieces, halves=halves)
    return pl.pallas_call(
        kernel,
        out_shape=jax.ShapeDtypeStruct((n_pieces, k_count, halves * tile), jnp.float32),
        grid=(n_pieces,),
        in_specs=[pl.BlockSpec(memory_space=pltpu.SMEM)]
        + [pl.BlockSpec((kr, width), lambda c: (0, 0)) for _ in range(pieces)]
        + [pl.BlockSpec((width, tile), lambda c: (0, 0)) for _ in columns],
        out_specs=pl.BlockSpec((1, k_count, halves * tile), lambda c: (c, 0, 0)),
        compiler_params=pltpu.CompilerParams(vmem_limit_bytes=48 * 1024 * 1024),
        cost_estimate=pl.CostEstimate(
            flops=2 * pieces * kr * width * total + 2 * pieces * kr * total,
            bytes_accessed=pieces * kr * width * 2 + width * total * 2 + k_count * total * 4,
            transcendentals=0,
        ),
    )(row_starts, *tensors, *columns)


def ring_pieces(x, axis):
    count = lax.axis_size(axis)
    return [x] + [
        lax.ppermute(x, axis, [(i, (i + d) % count) for i in range(count)]) for d in range(1, count)
    ]


def ring_sum_back(partial, axis):
    count = lax.axis_size(axis)
    total = partial[0]
    for d in range(1, count):
        total = total + lax.ppermute(partial[d], axis, [(i, (i - d) % count) for i in range(count)])
    return total


def swap_pair(x):
    return lax.ppermute(x, "mc", [(0, 1), (1, 0)])


def in_core_order(first_core, mine, other, axis):
    a = jnp.concatenate([mine, other], axis=axis)
    b = jnp.concatenate([other, mine], axis=axis)
    return jnp.where(first_core, a, b)


def per_device(density, tensor, velocity, inflow, flags):
    rows, depth, cells = density.shape
    position = lax.axis_index(SPACE)
    final = lax.axis_size(SPACE) - 1
    ghost_low = flags[0].astype(jnp.float32)[None, :] * inflow[:, None]
    ghost_high = flags[1].astype(jnp.float32)[None, :] * inflow[:, None]

    count = lax.axis_size(SPACE)
    halo_from = lambda d: lax.ppermute(
        density, SPACE, [(i, i + d) for i in range(max(0, -d), min(count, count - d))]
    )
    halos = [halo_from(2), halo_from(1), halo_from(-1), halo_from(-2)]
    halos, tensor = lax.optimization_barrier((halos, tensor))
    k_count, i_count, width = tensor.shape
    tensors = ring_pieces(tensor.reshape(k_count * i_count, width), "sy")
    field = run_transport(
        position.reshape(1).astype(jnp.int32),
        halos[0],
        halos[1],
        density,
        halos[2],
        halos[3],
        velocity[:, :, None],
        ghost_low,
        ghost_high,
        count * depth,
    )

    coarse = field.astype(jnp.bfloat16)
    all_modes = lax.all_gather(coarse, MODE, axis=0, tiled=True)
    first_core = lax.axis_index("mc") == 0
    mine = jnp.where(first_core, all_modes[:, 0], all_modes[:, 1])
    fetched = ring_pieces(mine, "sx")[1:]
    fetched, tensors = lax.optimization_barrier((fetched, tensors))
    other = swap_pair(jnp.stack(fetched))
    columns = [all_modes[:, 0], all_modes[:, 1]]
    for d in range(len(fetched)):
        columns.append(jnp.where(first_core, fetched[d], other[d]))
        columns.append(jnp.where(first_core, other[d], fetched[d]))

    sx = lax.axis_index("sx")
    sy = lax.axis_index("sy")
    ny = lax.axis_size("sy")
    row_starts = jnp.stack([(sx * ny + (sy - d) % ny) * i_count for d in range(ny)]).astype(jnp.int32)
    partial = contract(row_starts, tensors, columns, k_count, depth)
    gain = ring_sum_back(partial, "sx")
    return field + time_step * gain.reshape(field.shape)


def solution(mesh):
    devices = mesh.devices
    space, mode = devices.shape
    fine = Mesh(devices.reshape(4, space // 4, mode // 2, 2), SPACE + MODE)
    in_specs = (P(MODE, SPACE, None), P(MODE, SPACE, None), P(None, MODE), P(MODE), P())
    out_specs = P(MODE, SPACE, None)
    return jax.shard_map(
        per_device, mesh=fine, in_specs=in_specs, out_specs=out_specs, check_vma=False
    )
```

```python
import functools

import jax
import jax.numpy as jnp
from jax import lax
from jax.experimental import pallas as pl
from jax.experimental.pallas import tpu as pltpu
from jax.sharding import Mesh
from jax.sharding import PartitionSpec as P

NXY = 16
SUBSTEPS = 3
HALO = SUBSTEPS

courant = 0.3
time_step = 0.5


SPACE = ("sx", "sy")
MODE = ("mz", "mc")


def neighbours(field):
    rows, planes, cells = field.shape
    grid = field.reshape(rows, planes, NXY, NXY)
    padded = jnp.pad(grid, ((0, 0), (0, 0), (1, 1), (1, 1)))
    lower_x = padded[:, :, :-2, 1:-1].reshape(field.shape)
    upper_x = padded[:, :, 2:, 1:-1].reshape(field.shape)
    lower_y = padded[:, :, 1:-1, :-2].reshape(field.shape)
    upper_y = padded[:, :, 1:-1, 2:].reshape(field.shape)
    return (lower_x, upper_x, lower_y, upper_y)


def upwind(field, below, above, velocity):
    lower_x, upper_x, lower_y, upper_y = neighbours(field)
    lowers = [lower_x, lower_y, below]
    uppers = [upper_x, upper_y, above]
    flux = jnp.zeros_like(field)
    for direction in range(3):
        speed = velocity[direction][:, None, None]
        flux = flux + jnp.maximum(speed, 0.0) * (field - lowers[direction])
        flux = flux + jnp.minimum(speed, 0.0) * (uppers[direction] - field)
    return field - courant * flux


def with_halo(block, sides, width):
    for axis, dim in sides:
        count = lax.axis_size(axis)
        forward = [(i, i + 1) for i in range(count - 1)]
        backward = [(target, source) for source, target in forward]
        low = lax.ppermute(
            lax.slice_in_dim(block, block.shape[dim] - width, None, axis=dim), axis, forward
        )
        high = lax.ppermute(lax.slice_in_dim(block, 0, width, axis=dim), axis, backward)
        block = jnp.concatenate([low, block, high], axis=dim)
    return block


def plane_step(f, lower_z, upper_z, vel, x_lo, x_hi, y_lo, y_hi):
    cells = f.shape[-1]
    zero = jnp.zeros_like(f)
    lower_x = jnp.where(x_lo, zero, pltpu.roll(f, NXY, 1))
    upper_x = jnp.where(x_hi, zero, pltpu.roll(f, cells - NXY, 1))
    lower_y = jnp.where(y_lo, zero, pltpu.roll(f, 1, 1))
    upper_y = jnp.where(y_hi, zero, pltpu.roll(f, cells - 1, 1))
    lowers = [lower_x, lower_y, lower_z]
    uppers = [upper_x, upper_y, upper_z]
    flux = jnp.zeros_like(f)
    for direction in range(3):
        speed = vel[direction]
        flux = flux + jnp.maximum(speed, 0.0) * (f - lowers[direction])
        flux = flux + jnp.minimum(speed, 0.0) * (uppers[direction] - f)
    return f - courant * flux


def transport_kernel(pos_ref, b2_ref, b1_ref, d_ref, a1_ref, a2_ref, v_ref, gl_ref, gh_ref, o_ref, *, total_planes):
    depth = d_ref.shape[1]
    halo = SUBSTEPS
    extra = halo - depth
    planes = [b2_ref[:, depth - extra + i, :] for i in range(extra)]
    planes += [b1_ref[:, p, :] for p in range(depth)]
    planes += [d_ref[:, p, :] for p in range(depth)]
    planes += [a1_ref[:, p, :] for p in range(depth)]
    planes += [a2_ref[:, i, :] for i in range(extra)]
    rows, cells = planes[0].shape
    pos = pos_ref[0]
    gl = gl_ref[...]
    gh = gh_ref[...]
    vel = [v_ref[d] for d in range(3)]
    lane = lax.broadcasted_iota(jnp.int32, (rows, cells), 1)
    y = lane % NXY
    x = lane // NXY
    x_lo, x_hi, y_lo, y_hi = x == 0, x == NXY - 1, y == 0, y == NXY - 1

    def fix(e, f):
        z = pos * depth - halo + e
        f = jnp.where(z < 0, gl, f)
        return jnp.where(z >= total_planes, gh, f)

    field = [fix(e, f) for e, f in enumerate(planes)]
    n = len(field)
    for t in range(1, SUBSTEPS + 1):
        new = [None] * n
        for e in range(t, n - t):
            new[e] = fix(e, plane_step(field[e], field[e - 1], field[e + 1], vel, x_lo, x_hi, y_lo, y_hi))
        field = new
    for p in range(depth):
        o_ref[:, p, :] = field[halo + p]


def run_transport(pos, b2, b1, d, a1, a2, vel3, gl, gh, total_planes):
    rows, depth, cells = d.shape
    vmem = pltpu.VMEM
    spec = pl.BlockSpec(memory_space=vmem)
    return pl.pallas_call(
        functools.partial(transport_kernel, total_planes=total_planes),
        out_shape=jax.ShapeDtypeStruct(d.shape, d.dtype),
        in_specs=[pl.BlockSpec(memory_space=pltpu.SMEM)] + [spec] * 8,
        out_specs=spec,
    )(pos, b2, b1, d, a1, a2, vel3, gl, gh)


def gain_kernel(row_ref, *refs, group, rows, pieces, halves):
    t_refs = refs[:pieces]
    n_x = len(refs) - pieces - 1
    x_refs = refs[pieces : pieces + n_x]
    o_ref = refs[pieces + n_x]
    n_groups = o_ref.shape[1] // group
    column = pl.program_id(0)

    def run(x_group):
        x = jnp.concatenate([r[...] for r in x_group], axis=1)
        tile = x.shape[-1]
        xis = [
            jnp.concatenate(
                [r[pl.ds(pl.multiple_of(row_ref[d], rows), rows), :] for r in x_group], axis=1
            ).astype(jnp.float32)
            for d in range(pieces)
        ]

        def body(g, carry):
            start = pl.multiple_of(g * group * rows, group * rows)
            acc = None
            for d in range(pieces):
                t = t_refs[d][pl.ds(start, group * rows), :]
                inner = jnp.dot(t, x, preferred_element_type=jnp.float32)
                inner = inner.reshape(group, rows, tile)
                term = jnp.sum(inner * xis[d][None], axis=1)
                acc = term if acc is None else acc + term
            o_ref[0, pl.ds(pl.multiple_of(g * group, group), group), :] = acc
            return carry

        lax.fori_loop(0, n_groups, body, 0)

    for p in range(n_x // halves):
        group_refs = x_refs[p * halves : (p + 1) * halves]
        pl.when(column == p)(functools.partial(run, group_refs))


def contract(row_starts, tensors, columns, k_count, halves, group=32):
    kr, width = tensors[0].shape
    pieces = len(tensors)
    rows = kr // k_count
    tile = columns[0].shape[1]
    n_pieces = len(columns) // halves
    total = tile * len(columns)
    kernel = functools.partial(gain_kernel, group=group, rows=rows, pieces=pieces, halves=halves)
    return pl.pallas_call(
        kernel,
        out_shape=jax.ShapeDtypeStruct((n_pieces, k_count, halves * tile), jnp.float32),
        grid=(n_pieces,),
        in_specs=[pl.BlockSpec(memory_space=pltpu.SMEM)]
        + [pl.BlockSpec((kr, width), lambda c: (0, 0)) for _ in range(pieces)]
        + [pl.BlockSpec((width, tile), lambda c: (0, 0)) for _ in columns],
        out_specs=pl.BlockSpec((1, k_count, halves * tile), lambda c: (c, 0, 0)),
        compiler_params=pltpu.CompilerParams(vmem_limit_bytes=48 * 1024 * 1024),
        cost_estimate=pl.CostEstimate(
            flops=2 * pieces * kr * width * total + 2 * pieces * kr * total,
            bytes_accessed=pieces * kr * width * 2 + width * total * 2 + k_count * total * 4,
            transcendentals=0,
        ),
    )(row_starts, *tensors, *columns)


def ring_pieces(x, axis):
    count = lax.axis_size(axis)
    return [x] + [
        lax.ppermute(x, axis, [(i, (i + d) % count) for i in range(count)]) for d in range(1, count)
    ]


def ring_sum_back(partial, axis):
    count = lax.axis_size(axis)
    total = partial[0]
    for d in range(1, count):
        total = total + lax.ppermute(partial[d], axis, [(i, (i - d) % count) for i in range(count)])
    return total


def swap_pair(x):
    return lax.ppermute(x, "mc", [(0, 1), (1, 0)])


def in_core_order(first_core, mine, other, axis):
    a = jnp.concatenate([mine, other], axis=axis)
    b = jnp.concatenate([other, mine], axis=axis)
    return jnp.where(first_core, a, b)


def per_device(density, tensor, velocity, inflow, flags):
    rows, depth, cells = density.shape
    position = lax.axis_index(SPACE)
    final = lax.axis_size(SPACE) - 1
    ghost_low = flags[0].astype(jnp.float32)[None, :] * inflow[:, None]
    ghost_high = flags[1].astype(jnp.float32)[None, :] * inflow[:, None]

    count = lax.axis_size(SPACE)
    halo_from = lambda d: lax.ppermute(
        density, SPACE, [(i, i + d) for i in range(max(0, -d), min(count, count - d))]
    )
    halos = [halo_from(2), halo_from(1), halo_from(-1), halo_from(-2)]
    halos, tensor = lax.optimization_barrier((halos, tensor))
    k_count, i_count, width = tensor.shape
    tensors = ring_pieces(tensor.reshape(k_count * i_count, width), "sy")
    field = run_transport(
        position.reshape(1).astype(jnp.int32),
        halos[0],
        halos[1],
        density,
        halos[2],
        halos[3],
        velocity[:, :, None],
        ghost_low,
        ghost_high,
        count * depth,
    )

    coarse = field.astype(jnp.bfloat16)
    all_modes = lax.all_gather(coarse, MODE, axis=0, tiled=True)
    first_core = lax.axis_index("mc") == 0
    mine = jnp.where(first_core, all_modes[:, 0], all_modes[:, 1])
    fetched = ring_pieces(mine, "sx")[1:]
    fetched, tensors = lax.optimization_barrier((fetched, tensors))
    other = swap_pair(jnp.stack(fetched))
    columns = [mine, jnp.where(first_core, all_modes[:, 1], all_modes[:, 0])]
    for d in range(len(fetched)):
        columns += [fetched[d], other[d]]

    sx = lax.axis_index("sx")
    sy = lax.axis_index("sy")
    ny = lax.axis_size("sy")
    row_starts = jnp.stack([(sx * ny + (sy - d) % ny) * i_count for d in range(ny)]).astype(jnp.int32)
    partial = contract(row_starts, tensors, columns, k_count, depth)
    gain = ring_sum_back(partial, "sx")
    first, second = gain[:, :cells], gain[:, cells:]
    gain = jnp.stack(
        [jnp.where(first_core, first, second), jnp.where(first_core, second, first)], axis=1
    )
    return field + time_step * gain


def solution(mesh):
    devices = mesh.devices
    space, mode = devices.shape
    fine = Mesh(devices.reshape(4, space // 4, mode // 2, 2), SPACE + MODE)
    in_specs = (P(MODE, SPACE, None), P(MODE, SPACE, None), P(None, MODE), P(MODE), P())
    out_specs = P(MODE, SPACE, None)
    return jax.shard_map(
        per_device, mesh=fine, in_specs=in_specs, out_specs=out_specs, check_vma=False
    )
```

```python
import functools

import jax
import jax.numpy as jnp
from jax import lax
from jax.experimental import pallas as pl
from jax.experimental.pallas import tpu as pltpu
from jax.sharding import Mesh
from jax.sharding import PartitionSpec as P

NXY = 16
SUBSTEPS = 3
HALO = SUBSTEPS

courant = 0.3
time_step = 0.5


SPACE = ("sx", "sy")
MODE = ("mz", "mc")


def neighbours(field):
    rows, planes, cells = field.shape
    grid = field.reshape(rows, planes, NXY, NXY)
    padded = jnp.pad(grid, ((0, 0), (0, 0), (1, 1), (1, 1)))
    lower_x = padded[:, :, :-2, 1:-1].reshape(field.shape)
    upper_x = padded[:, :, 2:, 1:-1].reshape(field.shape)
    lower_y = padded[:, :, 1:-1, :-2].reshape(field.shape)
    upper_y = padded[:, :, 1:-1, 2:].reshape(field.shape)
    return (lower_x, upper_x, lower_y, upper_y)


def upwind(field, below, above, velocity):
    lower_x, upper_x, lower_y, upper_y = neighbours(field)
    lowers = [lower_x, lower_y, below]
    uppers = [upper_x, upper_y, above]
    flux = jnp.zeros_like(field)
    for direction in range(3):
        speed = velocity[direction][:, None, None]
        flux = flux + jnp.maximum(speed, 0.0) * (field - lowers[direction])
        flux = flux + jnp.minimum(speed, 0.0) * (uppers[direction] - field)
    return field - courant * flux


def with_halo(block, sides, width):
    for axis, dim in sides:
        count = lax.axis_size(axis)
        forward = [(i, i + 1) for i in range(count - 1)]
        backward = [(target, source) for source, target in forward]
        low = lax.ppermute(
            lax.slice_in_dim(block, block.shape[dim] - width, None, axis=dim), axis, forward
        )
        high = lax.ppermute(lax.slice_in_dim(block, 0, width, axis=dim), axis, backward)
        block = jnp.concatenate([low, block, high], axis=dim)
    return block


def plane_step(f, lower_z, upper_z, vel, x_lo, x_hi, y_lo, y_hi):
    cells = f.shape[-1]
    zero = jnp.zeros_like(f)
    lower_x = jnp.where(x_lo, zero, pltpu.roll(f, NXY, 1))
    upper_x = jnp.where(x_hi, zero, pltpu.roll(f, cells - NXY, 1))
    lower_y = jnp.where(y_lo, zero, pltpu.roll(f, 1, 1))
    upper_y = jnp.where(y_hi, zero, pltpu.roll(f, cells - 1, 1))
    lowers = [lower_x, lower_y, lower_z]
    uppers = [upper_x, upper_y, upper_z]
    flux = jnp.zeros_like(f)
    for direction in range(3):
        speed = vel[direction]
        flux = flux + jnp.maximum(speed, 0.0) * (f - lowers[direction])
        flux = flux + jnp.minimum(speed, 0.0) * (uppers[direction] - f)
    return f - courant * flux


def transport_kernel(pos_ref, b2_ref, b1_ref, d_ref, a1_ref, a2_ref, v_ref, fl_ref, o_ref, *, total_planes):
    depth = d_ref.shape[1]
    halo = SUBSTEPS
    extra = halo - depth
    planes = [b2_ref[:, depth - extra + i, :] for i in range(extra)]
    planes += [b1_ref[:, p, :] for p in range(depth)]
    planes += [d_ref[:, p, :] for p in range(depth)]
    planes += [a1_ref[:, p, :] for p in range(depth)]
    planes += [a2_ref[:, i, :] for i in range(extra)]
    rows, cells = planes[0].shape
    pos = pos_ref[0]
    flags = fl_ref[...].astype(jnp.float32)
    inflow = v_ref[3]
    gl = flags[0:1, :] * inflow
    gh = flags[1:2, :] * inflow
    vel = [v_ref[d] for d in range(3)]
    lane = lax.broadcasted_iota(jnp.int32, (rows, cells), 1)
    y = lane % NXY
    x = lane // NXY
    x_lo, x_hi, y_lo, y_hi = x == 0, x == NXY - 1, y == 0, y == NXY - 1

    def fix(e, f):
        z = pos * depth - halo + e
        f = jnp.where(z < 0, gl, f)
        return jnp.where(z >= total_planes, gh, f)

    field = [fix(e, f) for e, f in enumerate(planes)]
    n = len(field)
    for t in range(1, SUBSTEPS + 1):
        new = [None] * n
        for e in range(t, n - t):
            new[e] = fix(e, plane_step(field[e], field[e - 1], field[e + 1], vel, x_lo, x_hi, y_lo, y_hi))
        field = new
    for p in range(depth):
        o_ref[:, p, :] = field[halo + p]


def run_transport(pos, b2, b1, d, a1, a2, vel3, flags, total_planes):
    rows, depth, cells = d.shape
    vmem = pltpu.VMEM
    spec = pl.BlockSpec(memory_space=vmem)
    return pl.pallas_call(
        functools.partial(transport_kernel, total_planes=total_planes),
        out_shape=jax.ShapeDtypeStruct(d.shape, d.dtype),
        in_specs=[pl.BlockSpec(memory_space=pltpu.SMEM)] + [spec] * 7,
        out_specs=spec,
    )(pos, b2, b1, d, a1, a2, vel3, flags)


def gain_kernel(row_ref, *refs, group, rows, pieces, halves):
    t_refs = refs[:pieces]
    n_x = len(refs) - pieces - 1
    x_refs = refs[pieces : pieces + n_x]
    o_ref = refs[pieces + n_x]
    n_groups = o_ref.shape[1] // group
    column = pl.program_id(0)

    def run(x_group):
        x = jnp.concatenate([r[...] for r in x_group], axis=1)
        tile = x.shape[-1]
        xis = [
            jnp.concatenate(
                [r[pl.ds(pl.multiple_of(row_ref[d], rows), rows), :] for r in x_group], axis=1
            ).astype(jnp.float32)
            for d in range(pieces)
        ]

        def body(g, carry):
            start = pl.multiple_of(g * group * rows, group * rows)
            acc = None
            for d in range(pieces):
                t = t_refs[d][pl.ds(start, group * rows), :]
                inner = jnp.dot(t, x, preferred_element_type=jnp.float32)
                inner = inner.reshape(group, rows, tile)
                term = jnp.sum(inner * xis[d][None], axis=1)
                acc = term if acc is None else acc + term
            o_ref[0, pl.ds(pl.multiple_of(g * group, group), group), :] = acc
            return carry

        lax.fori_loop(0, n_groups, body, 0)

    for p in range(n_x // halves):
        group_refs = x_refs[p * halves : (p + 1) * halves]
        pl.when(column == p)(functools.partial(run, group_refs))


def contract(row_starts, tensors, columns, k_count, halves, group=32):
    kr, width = tensors[0].shape
    pieces = len(tensors)
    rows = kr // k_count
    tile = columns[0].shape[1]
    n_pieces = len(columns) // halves
    total = tile * len(columns)
    kernel = functools.partial(gain_kernel, group=group, rows=rows, pieces=pieces, halves=halves)
    return pl.pallas_call(
        kernel,
        out_shape=jax.ShapeDtypeStruct((n_pieces, k_count, halves * tile), jnp.float32),
        grid=(n_pieces,),
        in_specs=[pl.BlockSpec(memory_space=pltpu.SMEM)]
        + [pl.BlockSpec((kr, width), lambda c: (0, 0)) for _ in range(pieces)]
        + [pl.BlockSpec((width, tile), lambda c: (0, 0)) for _ in columns],
        out_specs=pl.BlockSpec((1, k_count, halves * tile), lambda c: (c, 0, 0)),
        compiler_params=pltpu.CompilerParams(vmem_limit_bytes=48 * 1024 * 1024),
        cost_estimate=pl.CostEstimate(
            flops=2 * pieces * kr * width * total + 2 * pieces * kr * total,
            bytes_accessed=pieces * kr * width * 2 + width * total * 2 + k_count * total * 4,
            transcendentals=0,
        ),
    )(row_starts, *tensors, *columns)


def ring_pieces(x, axis):
    count = lax.axis_size(axis)
    return [x] + [
        lax.ppermute(x, axis, [(i, (i + d) % count) for i in range(count)]) for d in range(1, count)
    ]


def ring_sum_back(partial, axis):
    count = lax.axis_size(axis)
    total = partial[0]
    for d in range(1, count):
        total = total + lax.ppermute(partial[d], axis, [(i, (i - d) % count) for i in range(count)])
    return total


def swap_pair(x):
    return lax.ppermute(x, "mc", [(0, 1), (1, 0)])


def in_core_order(first_core, mine, other, axis):
    a = jnp.concatenate([mine, other], axis=axis)
    b = jnp.concatenate([other, mine], axis=axis)
    return jnp.where(first_core, a, b)


def per_device(density, tensor, velocity, inflow, flags):
    rows, depth, cells = density.shape
    position = lax.axis_index(SPACE)
    final = lax.axis_size(SPACE) - 1

    count = lax.axis_size(SPACE)
    halo_from = lambda d: lax.ppermute(
        density, SPACE, [(i, i + d) for i in range(max(0, -d), min(count, count - d))]
    )
    halos = [halo_from(2), halo_from(1), halo_from(-1), halo_from(-2)]
    halos, tensor = lax.optimization_barrier((halos, tensor))
    k_count, i_count, width = tensor.shape
    tensors = ring_pieces(tensor.reshape(k_count * i_count, width), "sy")
    field = run_transport(
        position.reshape(1).astype(jnp.int32),
        halos[0],
        halos[1],
        density,
        halos[2],
        halos[3],
        jnp.concatenate([velocity, inflow[None]], axis=0)[:, :, None],
        flags,
        count * depth,
    )

    coarse = field.astype(jnp.bfloat16)
    all_modes = lax.all_gather(coarse, MODE, axis=0, tiled=True)
    first_core = lax.axis_index("mc") == 0
    mine = jnp.where(first_core, all_modes[:, 0], all_modes[:, 1])
    fetched = ring_pieces(mine, "sx")[1:]
    fetched, tensors = lax.optimization_barrier((fetched, tensors))
    other = swap_pair(jnp.stack(fetched))
    columns = [all_modes[:, 0], all_modes[:, 1]]
    for d in range(len(fetched)):
        columns.append(jnp.where(first_core, fetched[d], other[d]))
        columns.append(jnp.where(first_core, other[d], fetched[d]))

    sx = lax.axis_index("sx")
    sy = lax.axis_index("sy")
    ny = lax.axis_size("sy")
    row_starts = jnp.stack([(sx * ny + (sy - d) % ny) * i_count for d in range(ny)]).astype(jnp.int32)
    partial = contract(row_starts, tensors, columns, k_count, depth)
    gain = ring_sum_back(partial, "sx")
    return field + time_step * gain.reshape(field.shape)


def solution(mesh):
    devices = mesh.devices
    space, mode = devices.shape
    fine = Mesh(devices.reshape(4, space // 4, mode // 2, 2), SPACE + MODE)
    in_specs = (P(MODE, SPACE, None), P(MODE, SPACE, None), P(None, MODE), P(MODE), P())
    out_specs = P(MODE, SPACE, None)
    return jax.shard_map(
        per_device, mesh=fine, in_specs=in_specs, out_specs=out_specs, check_vma=False
    )
```

```python
import functools

import jax
import jax.numpy as jnp
from jax import lax
from jax.experimental import pallas as pl
from jax.experimental.pallas import tpu as pltpu
from jax.sharding import Mesh
from jax.sharding import PartitionSpec as P

NXY = 16
SUBSTEPS = 3
HALO = SUBSTEPS

courant = 0.3
time_step = 0.5


SPACE = ("sx", "sy")
MODE = ("mz", "mc")


def neighbours(field):
    rows, planes, cells = field.shape
    grid = field.reshape(rows, planes, NXY, NXY)
    padded = jnp.pad(grid, ((0, 0), (0, 0), (1, 1), (1, 1)))
    lower_x = padded[:, :, :-2, 1:-1].reshape(field.shape)
    upper_x = padded[:, :, 2:, 1:-1].reshape(field.shape)
    lower_y = padded[:, :, 1:-1, :-2].reshape(field.shape)
    upper_y = padded[:, :, 1:-1, 2:].reshape(field.shape)
    return (lower_x, upper_x, lower_y, upper_y)


def upwind(field, below, above, velocity):
    lower_x, upper_x, lower_y, upper_y = neighbours(field)
    lowers = [lower_x, lower_y, below]
    uppers = [upper_x, upper_y, above]
    flux = jnp.zeros_like(field)
    for direction in range(3):
        speed = velocity[direction][:, None, None]
        flux = flux + jnp.maximum(speed, 0.0) * (field - lowers[direction])
        flux = flux + jnp.minimum(speed, 0.0) * (uppers[direction] - field)
    return field - courant * flux


def with_halo(block, sides, width):
    for axis, dim in sides:
        count = lax.axis_size(axis)
        forward = [(i, i + 1) for i in range(count - 1)]
        backward = [(target, source) for source, target in forward]
        low = lax.ppermute(
            lax.slice_in_dim(block, block.shape[dim] - width, None, axis=dim), axis, forward
        )
        high = lax.ppermute(lax.slice_in_dim(block, 0, width, axis=dim), axis, backward)
        block = jnp.concatenate([low, block, high], axis=dim)
    return block


def plane_step(f, lower_z, upper_z, vel, x_lo, x_hi, y_lo, y_hi):
    cells = f.shape[-1]
    zero = jnp.zeros_like(f)
    lower_x = jnp.where(x_lo, zero, pltpu.roll(f, NXY, 1))
    upper_x = jnp.where(x_hi, zero, pltpu.roll(f, cells - NXY, 1))
    lower_y = jnp.where(y_lo, zero, pltpu.roll(f, 1, 1))
    upper_y = jnp.where(y_hi, zero, pltpu.roll(f, cells - 1, 1))
    lowers = [lower_x, lower_y, lower_z]
    uppers = [upper_x, upper_y, upper_z]
    flux = jnp.zeros_like(f)
    for direction in range(3):
        speed = vel[direction]
        flux = flux + jnp.maximum(speed, 0.0) * (f - lowers[direction])
        flux = flux + jnp.minimum(speed, 0.0) * (uppers[direction] - f)
    return f - courant * flux


def transport_kernel(pos_ref, b2_ref, b1_ref, d_ref, a1_ref, a2_ref, v_ref, fl_ref, o_ref, c_ref, *, total_planes):
    depth = d_ref.shape[1]
    halo = SUBSTEPS
    extra = halo - depth
    planes = [b2_ref[:, depth - extra + i, :] for i in range(extra)]
    planes += [b1_ref[:, p, :] for p in range(depth)]
    planes += [d_ref[:, p, :] for p in range(depth)]
    planes += [a1_ref[:, p, :] for p in range(depth)]
    planes += [a2_ref[:, i, :] for i in range(extra)]
    rows, cells = planes[0].shape
    pos = pos_ref[0]
    flags = fl_ref[...].astype(jnp.float32)
    inflow = v_ref[3]
    gl = flags[0:1, :] * inflow
    gh = flags[1:2, :] * inflow
    vel = [v_ref[d] for d in range(3)]
    lane = lax.broadcasted_iota(jnp.int32, (rows, cells), 1)
    y = lane % NXY
    x = lane // NXY
    x_lo, x_hi, y_lo, y_hi = x == 0, x == NXY - 1, y == 0, y == NXY - 1

    def fix(e, f):
        z = pos * depth - halo + e
        f = jnp.where(z < 0, gl, f)
        return jnp.where(z >= total_planes, gh, f)

    field = [fix(e, f) for e, f in enumerate(planes)]
    n = len(field)
    for t in range(1, SUBSTEPS + 1):
        new = [None] * n
        for e in range(t, n - t):
            new[e] = fix(e, plane_step(field[e], field[e - 1], field[e + 1], vel, x_lo, x_hi, y_lo, y_hi))
        field = new
    for p in range(depth):
        o_ref[:, p, :] = field[halo + p]
        c_ref[:, p, :] = field[halo + p].astype(c_ref.dtype)


def run_transport(pos, b2, b1, d, a1, a2, vel3, flags, total_planes):
    rows, depth, cells = d.shape
    vmem = pltpu.VMEM
    spec = pl.BlockSpec(memory_space=vmem)
    return pl.pallas_call(
        functools.partial(transport_kernel, total_planes=total_planes),
        out_shape=(jax.ShapeDtypeStruct(d.shape, d.dtype), jax.ShapeDtypeStruct(d.shape, jnp.bfloat16)),
        in_specs=[pl.BlockSpec(memory_space=pltpu.SMEM)] + [spec] * 7,
        out_specs=(spec, spec),
    )(pos, b2, b1, d, a1, a2, vel3, flags)


def gain_kernel(row_ref, *refs, group, rows, pieces, halves):
    t_refs = refs[:pieces]
    n_x = len(refs) - pieces - 1
    x_refs = refs[pieces : pieces + n_x]
    o_ref = refs[pieces + n_x]
    n_groups = o_ref.shape[1] // group
    column = pl.program_id(0)

    def run(x_group):
        x = jnp.concatenate([r[...] for r in x_group], axis=1)
        tile = x.shape[-1]
        xis = [
            jnp.concatenate(
                [r[pl.ds(pl.multiple_of(row_ref[d], rows), rows), :] for r in x_group], axis=1
            ).astype(jnp.float32)
            for d in range(pieces)
        ]

        def body(g, carry):
            start = pl.multiple_of(g * group * rows, group * rows)
            acc = None
            for d in range(pieces):
                t = t_refs[d][pl.ds(start, group * rows), :]
                inner = jnp.dot(t, x, preferred_element_type=jnp.float32)
                inner = inner.reshape(group, rows, tile)
                term = jnp.sum(inner * xis[d][None], axis=1)
                acc = term if acc is None else acc + term
            o_ref[0, pl.ds(pl.multiple_of(g * group, group), group), :] = acc
            return carry

        lax.fori_loop(0, n_groups, body, 0)

    for p in range(n_x // halves):
        group_refs = x_refs[p * halves : (p + 1) * halves]
        pl.when(column == p)(functools.partial(run, group_refs))


def contract(row_starts, tensors, columns, k_count, halves, group=32):
    kr, width = tensors[0].shape
    pieces = len(tensors)
    rows = kr // k_count
    tile = columns[0].shape[1]
    n_pieces = len(columns) // halves
    total = tile * len(columns)
    kernel = functools.partial(gain_kernel, group=group, rows=rows, pieces=pieces, halves=halves)
    return pl.pallas_call(
        kernel,
        out_shape=jax.ShapeDtypeStruct((n_pieces, k_count, halves * tile), jnp.float32),
        grid=(n_pieces,),
        in_specs=[pl.BlockSpec(memory_space=pltpu.SMEM)]
        + [pl.BlockSpec((kr, width), lambda c: (0, 0)) for _ in range(pieces)]
        + [pl.BlockSpec((width, tile), lambda c: (0, 0)) for _ in columns],
        out_specs=pl.BlockSpec((1, k_count, halves * tile), lambda c: (c, 0, 0)),
        compiler_params=pltpu.CompilerParams(vmem_limit_bytes=48 * 1024 * 1024),
        cost_estimate=pl.CostEstimate(
            flops=2 * pieces * kr * width * total + 2 * pieces * kr * total,
            bytes_accessed=pieces * kr * width * 2 + width * total * 2 + k_count * total * 4,
            transcendentals=0,
        ),
    )(row_starts, *tensors, *columns)


def ring_pieces(x, axis):
    count = lax.axis_size(axis)
    return [x] + [
        lax.ppermute(x, axis, [(i, (i + d) % count) for i in range(count)]) for d in range(1, count)
    ]


def ring_sum_back(partial, axis):
    count = lax.axis_size(axis)
    total = partial[0]
    for d in range(1, count):
        total = total + lax.ppermute(partial[d], axis, [(i, (i - d) % count) for i in range(count)])
    return total


def swap_pair(x):
    return lax.ppermute(x, "mc", [(0, 1), (1, 0)])


def in_core_order(first_core, mine, other, axis):
    a = jnp.concatenate([mine, other], axis=axis)
    b = jnp.concatenate([other, mine], axis=axis)
    return jnp.where(first_core, a, b)


def per_device(density, tensor, velocity, inflow, flags):
    rows, depth, cells = density.shape
    position = lax.axis_index(SPACE)
    final = lax.axis_size(SPACE) - 1

    count = lax.axis_size(SPACE)
    halo_from = lambda d: lax.ppermute(
        density, SPACE, [(i, i + d) for i in range(max(0, -d), min(count, count - d))]
    )
    halos = [halo_from(2), halo_from(1), halo_from(-1), halo_from(-2)]
    halos, tensor = lax.optimization_barrier((halos, tensor))
    k_count, i_count, width = tensor.shape
    tensors = ring_pieces(tensor.reshape(k_count * i_count, width), "sy")
    field, coarse = run_transport(
        position.reshape(1).astype(jnp.int32),
        halos[0],
        halos[1],
        density,
        halos[2],
        halos[3],
        jnp.concatenate([velocity, inflow[None]], axis=0)[:, :, None],
        flags,
        count * depth,
    )

    all_modes = lax.all_gather(coarse, MODE, axis=0, tiled=True)
    first_core = lax.axis_index("mc") == 0
    mine = jnp.where(first_core, all_modes[:, 0], all_modes[:, 1])
    fetched = ring_pieces(mine, "sx")[1:]
    fetched, tensors = lax.optimization_barrier((fetched, tensors))
    other = swap_pair(jnp.stack(fetched))
    columns = [all_modes[:, 0], all_modes[:, 1]]
    for d in range(len(fetched)):
        columns.append(jnp.where(first_core, fetched[d], other[d]))
        columns.append(jnp.where(first_core, other[d], fetched[d]))

    sx = lax.axis_index("sx")
    sy = lax.axis_index("sy")
    ny = lax.axis_size("sy")
    row_starts = jnp.stack([(sx * ny + (sy - d) % ny) * i_count for d in range(ny)]).astype(jnp.int32)
    partial = contract(row_starts, tensors, columns, k_count, depth)
    gain = ring_sum_back(partial, "sx")
    return field + time_step * gain.reshape(field.shape)


def solution(mesh):
    devices = mesh.devices
    space, mode = devices.shape
    fine = Mesh(devices.reshape(4, space // 4, mode // 2, 2), SPACE + MODE)
    in_specs = (P(MODE, SPACE, None), P(MODE, SPACE, None), P(None, MODE), P(MODE), P())
    out_specs = P(MODE, SPACE, None)
    return jax.shard_map(
        per_device, mesh=fine, in_specs=in_specs, out_specs=out_specs, check_vma=False
    )
```
